512 devices in a mesh: lat: 16 (over y, core), lon: 32 (over z, x).
Axes of the slice: x: 4, y: 8, z: 8, core: 2. Of those that a mesh axis runs over, the one named last changes fastest.
Arguments:
- tracers: bfloat16 [1, 512, 1440, 128], P(None, 'lat', 'lon'), may hold values from -6 to 6
- courant: float32 [512, 2, 1440, 128], P('lat', None, 'lon'), may hold values from -0.5 to 0.5
- row_mask: int32 [512], P('lat'), may hold values from 0 to 1, as said below
- damped_modes: int32 [512], P('lat'), may hold values from 180 to 720
- damping: float32 [512, 721], P('lat'), may hold values from 0.05 to 0.8
Outputs:
- advected: bfloat16 [1, 512, 1440, 128], P(None, 'lat', 'lon')
The draws below stay inside these ranges and needn't reach their ends.
Inputs may be any that keep to these rules, and one draw needn't show every extreme that they name: row_mask is 0 outside the first 128 and the last 128 latitude rows.
All inputs are finite; a program needn't handle non-finite values.
Results may differ from the reference program's by a relative error of at most 0.0052.
Values may be sent and summed in bfloat16 or wider, within the bound.
No kernel may reach another device: no remote copies, remote signals or barrier semaphores. Data moves between devices by JAX's collectives and lax.ppermute only.
A program may use at most 64 MiB of HBM per device.

```python
import math
import jax
import jax.numpy as jnp
from jax import lax

NLON = 1440
NK = 721
LEV = 128
NTRACER = 1
NLAT = 512


def draw_row_mask(key, part):
    latitude_rows = jnp.arange(NLAT, dtype=jnp.int32)
    polar_rows = NLAT // 4
    inside = (latitude_rows < polar_rows) | (latitude_rows >= NLAT - polar_rows)
    picks = jax.random.randint(key, (NLAT,), 0, 4)
    return jnp.where(inside & (picks > 0), 1, 0).astype(jnp.int32)


def with_ends(array, key, smallest, high):
    longest = array.shape.index(max(array.shape))
    spots = []
    for shift in (0, 1):
        where = [jax.random.randint(jax.random.fold_in(key, axis), (), 0, length) for axis, length in enumerate(array.shape)]
        where[longest] = (where[longest] + shift) % array.shape[longest]
        spots.append(tuple(where))
    return array.at[spots[0]].set(smallest).at[spots[1]].set(high)


def steps_of(rng, dims, pieces, low, top_value):
    loudness, own = 1.0, jax.random.fold_in(rng, 6)
    for axis_at, blocks in pieces:
        heights = jnp.exp(jax.random.uniform(jax.random.fold_in(own, axis_at), (blocks,), jnp.float32, low / len(pieces), top_value / len(pieces)))
        loudness = loudness * jnp.repeat(heights, dims[axis_at] // blocks).reshape([-1 if axis == axis_at else 1 for axis in range(len(dims))])
    return loudness


def gaussian(own_key, extent, scale, reach, pieces=(), held_as=jnp.bfloat16):
    factor_of = steps_of(own_key, extent, pieces, -0.22, 0.18) if pieces else 1.0
    result = jax.random.normal(own_key, extent, jnp.float32) * scale * factor_of
    return jnp.minimum(jnp.maximum(result, -reach), reach).astype(held_as)


def setup_inputs(seed: int = 0) -> dict:
    arg_keys = jax.random.split(jax.random.key(seed), 6)
    tracers = gaussian(arg_keys[0], (NTRACER, NLAT, NLON, LEV), 1.0, 6.0, ((1, 16), (2, 32)))
    courant = jnp.clip(jax.random.uniform(arg_keys[1], (NLAT, 2, NLON, LEV), jnp.float32, -0.5, 0.5) * steps_of(arg_keys[1], (NLAT, 2, NLON, LEV), ((0, 16), (2, 32)), -0.4, 0.0), -0.5, 0.5)
    row_mask = draw_row_mask(jax.random.fold_in(arg_keys[5], 71), 0)
    damped_modes = with_ends(jax.random.randint(arg_keys[3], (NLAT,), NK // 4, NK), jax.random.fold_in(arg_keys[3], 1), NK // 4, NK - 1).astype(jnp.int32)
    damping = jnp.clip(jnp.exp(math.log(0.8) - 2.7725887 * jax.random.uniform(arg_keys[4], (NLAT, NK), jnp.float32) ** steps_of(arg_keys[4], (NLAT, NK), ((0, 16),), -0.2, 0.2)), 0.05, 0.8)
    return {"tracers": tracers, "courant": courant, "row_mask": row_mask, "damped_modes": damped_modes, "damping": damping}


def take_slice(values, low_end, high_end, along_axis):
    return lax.slice_in_dim(values, low_end, high_end, axis=along_axis)


def ppm_change(extended, courant_faces, along_axis, count_cells):
    edge_values = (7.0 / 12.0) * (take_slice(extended, 1, count_cells + 4, along_axis) + take_slice(extended, 2, count_cells + 5, along_axis)) - (1.0 / 12.0) * (take_slice(extended, 0, count_cells + 3, along_axis) + take_slice(extended, 3, count_cells + 6, along_axis))
    left_edge = take_slice(edge_values, 0, count_cells + 2, along_axis)
    right_edge = take_slice(edge_values, 1, count_cells + 3, along_axis)
    centre = take_slice(extended, 2, count_cells + 4, along_axis)
    slope_edge = right_edge - left_edge
    curvature = 6.0 * (centre - 0.5 * (left_edge + right_edge))
    upwind_plus = courant_faces * (take_slice(right_edge, 0, count_cells + 1, along_axis) - 0.5 * courant_faces * (take_slice(slope_edge, 0, count_cells + 1, along_axis) - (1.0 - courant_faces * (2.0 / 3.0)) * take_slice(curvature, 0, count_cells + 1, along_axis)))
    upwind_minus = courant_faces * (take_slice(left_edge, 1, count_cells + 2, along_axis) - 0.5 * courant_faces * (take_slice(slope_edge, 1, count_cells + 2, along_axis) + (1.0 + courant_faces * (2.0 / 3.0)) * take_slice(curvature, 1, count_cells + 2, along_axis)))
    face_flux = jnp.where(courant_faces > 0, upwind_plus, upwind_minus)
    return take_slice(face_flux, 0, count_cells, along_axis) - take_slice(face_flux, 1, count_cells + 1, along_axis)


def filter_row(row_pair):
    row_winds, row_factor = row_pair
    spectrum = jnp.fft.rfft(row_winds, axis=1)
    return jnp.fft.irfft(spectrum * row_factor[None, :, None], n=NLON, axis=1)


def reference(tracers, courant, row_mask, damped_modes, damping):
    mode_index = jnp.arange(NK, dtype=jnp.int32)
    damped = (row_mask[:, None] == 1) & (mode_index[None, :] >= NK - damped_modes[:, None])
    factor = jnp.where(damped, damping, 1.0)
    filtered = lax.map(filter_row, (courant, factor)).astype(jnp.bfloat16)
    level_block = math.gcd(LEV, 8)
    block_count = LEV // level_block

    def advect_block(block_index):
        first_level = block_index * level_block
        tracer_block = lax.dynamic_slice_in_dim(tracers, first_level, level_block, axis=3).astype(jnp.float32)
        wind_block = lax.dynamic_slice_in_dim(filtered, first_level, level_block, axis=3).astype(jnp.float32)
        zonal_wind = wind_block[:, 0]
        meridional_wind = wind_block[:, 1]
        extended = jnp.concatenate([tracer_block[:, :, NLON - 3:], tracer_block, tracer_block[:, :, :3]], axis=2)
        zonal_faces = jnp.concatenate([zonal_wind, zonal_wind[:, :1]], axis=1)
        middle = (tracer_block + ppm_change(extended, zonal_faces[None], 2, NLON)).astype(jnp.bfloat16)
        middle_wide = middle.astype(jnp.float32)
        padded = jnp.pad(middle_wide, ((0, 0), (3, 3), (0, 0), (0, 0)))
        face_rows = jnp.arange(NLAT + 1, dtype=jnp.int32)[:, None, None]
        meridional_faces = jnp.concatenate([meridional_wind, jnp.zeros((1, NLON, level_block), jnp.float32)], axis=0)
        meridional_faces = jnp.where(face_rows > 0, meridional_faces, 0.0)
        return (middle_wide + ppm_change(padded, meridional_faces[None], 1, NLAT)).astype(jnp.bfloat16)

    stacked = lax.map(advect_block, jnp.arange(block_count, dtype=jnp.int32))
    return jnp.moveaxis(stacked, 0, 3).reshape(NTRACER, NLAT, NLON, LEV)
```

```python
import math

import jax
import jax.numpy as jnp
from jax import lax
from jax.sharding import PartitionSpec as P


def padded(value, sides, width, wrap):
    for axis, dim in sides:
        size, length = (lax.axis_size(axis), value.shape[dim])
        up = [(i, (i + 1) % size) for i in range(size if wrap else size - 1)]
        down = [(j, i) for i, j in up]
        last = lax.slice_in_dim(value, length - width, length, axis=dim)
        leading = lax.slice_in_dim(value, 0, width, axis=dim)
        before = lax.ppermute(last, axis, up)
        after = lax.ppermute(leading, axis, down)
        value = jnp.concatenate([before, value, after], axis=dim)
    return value


def take_slice(values, low_end, high_end, along_axis):
    return lax.slice_in_dim(values, low_end, high_end, axis=along_axis)


def ppm_change(extended, courant_faces, along_axis, count_cells):
    edge_values = 7.0 / 12.0 * (
        take_slice(extended, 1, count_cells + 4, along_axis)
        + take_slice(extended, 2, count_cells + 5, along_axis)
    ) - 1.0 / 12.0 * (
        take_slice(extended, 0, count_cells + 3, along_axis)
        + take_slice(extended, 3, count_cells + 6, along_axis)
    )
    left_edge = take_slice(edge_values, 0, count_cells + 2, along_axis)
    right_edge = take_slice(edge_values, 1, count_cells + 3, along_axis)
    centre = take_slice(extended, 2, count_cells + 4, along_axis)
    slope_edge = right_edge - left_edge
    curvature = 6.0 * (centre - 0.5 * (left_edge + right_edge))
    upwind_plus = courant_faces * (
        take_slice(right_edge, 0, count_cells + 1, along_axis)
        - 0.5
        * courant_faces
        * (
            take_slice(slope_edge, 0, count_cells + 1, along_axis)
            - (1.0 - courant_faces * (2.0 / 3.0))
            * take_slice(curvature, 0, count_cells + 1, along_axis)
        )
    )
    upwind_minus = courant_faces * (
        take_slice(left_edge, 1, count_cells + 2, along_axis)
        - 0.5
        * courant_faces
        * (
            take_slice(slope_edge, 1, count_cells + 2, along_axis)
            + (1.0 + courant_faces * (2.0 / 3.0))
            * take_slice(curvature, 1, count_cells + 2, along_axis)
        )
    )
    face_flux = jnp.where(courant_faces > 0, upwind_plus, upwind_minus)
    return take_slice(face_flux, 0, count_cells, along_axis) - take_slice(
        face_flux, 1, count_cells + 1, along_axis
    )


def spectral_basis(blocks, block_len, span, mode_count):
    total_lon = blocks * block_len
    scale = 2.0 * math.pi / total_lon
    mode_index = jnp.arange(mode_count, dtype=jnp.int32)[None, :]
    coarse = jnp.arange(blocks, dtype=jnp.int32)[:, None]
    fine = jnp.arange(span, dtype=jnp.int32)[:, None]
    coarse_angle = ((block_len * coarse * mode_index) % total_lon).astype(jnp.float32) * scale
    fine_angle = ((fine * mode_index) % total_lon).astype(jnp.float32) * scale
    cc, sc = jnp.cos(coarse_angle)[:, None, :], jnp.sin(coarse_angle)[:, None, :]
    cf, sf = jnp.cos(fine_angle)[None], jnp.sin(fine_angle)[None]
    cosine = cc * cf - sc * sf
    sine = sc * cf + cc * sf
    table = jnp.concatenate([cosine, -sine], axis=2)
    mode_weight = (
        jnp.where((mode_index[0] == 0) | (2 * mode_index[0] == total_lon), 1.0, 2.0) / total_lon
    )
    return table, jnp.concatenate([mode_weight, mode_weight], axis=0)


def filter_correction(courant, row_factor):
    row_count, _, lon_local, levels = courant.shape
    blocks = lax.axis_size("lon")
    mode_count = row_factor.shape[1]
    table, mode_weight = spectral_basis(blocks, lon_local, lon_local + 1, mode_count)
    forward_table = table[:, :lon_local].reshape(blocks * lon_local, 2 * mode_count).astype(jnp.bfloat16)
    inverse_table = table.astype(jnp.bfloat16)
    flattened = courant.reshape(2 * row_count, lon_local, levels).astype(jnp.bfloat16)
    pair_factor = jnp.repeat(1.0 - row_factor, 2, axis=0)
    removal = jnp.concatenate([pair_factor, pair_factor], axis=1) * mode_weight[None, :]
    per_device = 2 * row_count // blocks
    level_block = lax.all_to_all(flattened, "lon", split_axis=0, concat_axis=1, tiled=True)
    first_row = lax.axis_index("lon") * per_device
    local_removal = lax.dynamic_slice_in_dim(removal, first_row, per_device, 0)
    spectrum = jnp.einsum(
        "cnl,nm->cml", level_block, forward_table, preferred_element_type=jnp.float32
    )
    weighted = (spectrum * local_removal[:, :, None]).astype(jnp.bfloat16)
    correction = jnp.einsum(
        "cml,djm->dcjl", weighted, inverse_table, preferred_element_type=jnp.float32
    ).astype(jnp.bfloat16)
    returned = lax.all_to_all(correction, "lon", split_axis=0, concat_axis=0, tiled=True)
    return returned.reshape(row_count, 2, lon_local + 1, levels)


def local(tracers, courant, row_mask, damped_modes, damping):
    rows_local = courant.shape[0]
    lon_local = courant.shape[2]
    mode_count = damping.shape[1]
    tracer_count = tracers.shape[0]
    lon_size = lax.axis_size("lon")
    mode_index = jnp.arange(mode_count, dtype=jnp.int32)
    damped = (row_mask[:, None] == 1) & (mode_index[None, :] >= mode_count - damped_modes[:, None])
    factor = jnp.where(damped, damping, 1.0)
    tracer_wide = padded(tracers, (("lon", 2),), 3, True).astype(jnp.float32)
    east_column = lax.ppermute(
        courant[:, 0, 0:1], "lon", [(i, (i - 1) % lon_size) for i in range(lon_size)]
    )
    correction = filter_correction(courant, factor).astype(jnp.float32)
    zonal_courant = jnp.concatenate([courant[:, 0], east_column], axis=1)
    zonal_faces = (zonal_courant - correction[:, 0]).astype(jnp.bfloat16)
    meridional_filtered = (courant[:, 1] - correction[:, 1, :lon_local]).astype(jnp.bfloat16)
    middle = (
        tracers.astype(jnp.float32)
        + ppm_change(tracer_wide, zonal_faces.astype(jnp.float32)[None], 2, lon_local)
    ).astype(jnp.bfloat16)
    meridional_stack = jnp.concatenate([middle, meridional_filtered[None]], axis=0)
    meridional_band = padded(meridional_stack, (("lat", 1),), 3, False)
    middle_wide = meridional_band[:tracer_count].astype(jnp.float32)
    meridional_faces = meridional_band[tracer_count, 3 : rows_local + 4].astype(jnp.float32)
    face_rows = lax.axis_index("lat") * rows_local + jnp.arange(rows_local + 1, dtype=jnp.int32)
    meridional_faces = jnp.where(face_rows[:, None, None] > 0, meridional_faces, 0.0)
    return (
        middle.astype(jnp.float32) + ppm_change(middle_wide, meridional_faces[None], 1, rows_local)
    ).astype(jnp.bfloat16)


def solution(mesh):
    placed = (
        P(None, "lat", "lon", None),
        P("lat", None, "lon", None),
        P("lat"),
        P("lat"),
        P("lat", None),
    )
    return jax.shard_map(
        local, mesh=mesh, in_specs=placed, out_specs=P(None, "lat", "lon", None), check_vma=False
    )
```

```python
import math

import jax
import jax.numpy as jnp
from jax import lax
from jax.sharding import PartitionSpec as P


def padded(value, sides, width, wrap):
    for axis, dim in sides:
        size, length = (lax.axis_size(axis), value.shape[dim])
        up = [(i, (i + 1) % size) for i in range(size if wrap else size - 1)]
        down = [(j, i) for i, j in up]
        last = lax.slice_in_dim(value, length - width, length, axis=dim)
        leading = lax.slice_in_dim(value, 0, width, axis=dim)
        before = lax.ppermute(last, axis, up)
        after = lax.ppermute(leading, axis, down)
        value = jnp.concatenate([before, value, after], axis=dim)
    return value


def take_slice(values, low_end, high_end, along_axis):
    return lax.slice_in_dim(values, low_end, high_end, axis=along_axis)


def ppm_change(extended, courant_faces, along_axis, count_cells):
    edge_values = 7.0 / 12.0 * (
        take_slice(extended, 1, count_cells + 4, along_axis)
        + take_slice(extended, 2, count_cells + 5, along_axis)
    ) - 1.0 / 12.0 * (
        take_slice(extended, 0, count_cells + 3, along_axis)
        + take_slice(extended, 3, count_cells + 6, along_axis)
    )
    left_edge = take_slice(edge_values, 0, count_cells + 2, along_axis)
    right_edge = take_slice(edge_values, 1, count_cells + 3, along_axis)
    centre = take_slice(extended, 2, count_cells + 4, along_axis)
    slope_edge = right_edge - left_edge
    curvature = 6.0 * (centre - 0.5 * (left_edge + right_edge))
    upwind_plus = courant_faces * (
        take_slice(right_edge, 0, count_cells + 1, along_axis)
        - 0.5
        * courant_faces
        * (
            take_slice(slope_edge, 0, count_cells + 1, along_axis)
            - (1.0 - courant_faces * (2.0 / 3.0))
            * take_slice(curvature, 0, count_cells + 1, along_axis)
        )
    )
    upwind_minus = courant_faces * (
        take_slice(left_edge, 1, count_cells + 2, along_axis)
        - 0.5
        * courant_faces
        * (
            take_slice(slope_edge, 1, count_cells + 2, along_axis)
            + (1.0 + courant_faces * (2.0 / 3.0))
            * take_slice(curvature, 1, count_cells + 2, along_axis)
        )
    )
    face_flux = jnp.where(courant_faces > 0, upwind_plus, upwind_minus)
    return take_slice(face_flux, 0, count_cells, along_axis) - take_slice(
        face_flux, 1, count_cells + 1, along_axis
    )


def spectral_basis(blocks, block_len, span, mode_count):
    total_lon = blocks * block_len
    scale = 2.0 * math.pi / total_lon
    mode_index = jnp.arange(mode_count, dtype=jnp.int32)[None, :]
    coarse = jnp.arange(blocks, dtype=jnp.int32)[:, None]
    fine = jnp.arange(span, dtype=jnp.int32)[:, None]
    coarse_angle = ((block_len * coarse * mode_index) % total_lon).astype(jnp.float32) * scale
    fine_angle = ((fine * mode_index) % total_lon).astype(jnp.float32) * scale
    cc, sc = jnp.cos(coarse_angle)[:, None, :], jnp.sin(coarse_angle)[:, None, :]
    cf, sf = jnp.cos(fine_angle)[None], jnp.sin(fine_angle)[None]
    cosine = cc * cf - sc * sf
    sine = sc * cf + cc * sf
    table = jnp.concatenate([cosine, -sine], axis=2)
    mode_weight = (
        jnp.where((mode_index[0] == 0) | (2 * mode_index[0] == total_lon), 1.0, 2.0) / total_lon
    )
    return table, jnp.concatenate([mode_weight, mode_weight], axis=0)


def filter_correction(courant, row_factor):
    row_count, _, lon_local, levels = courant.shape
    blocks = lax.axis_size("lon")
    mode_count = row_factor.shape[1]
    per_device = 2 * row_count // blocks
    table, mode_weight = spectral_basis(blocks, lon_local, lon_local + 1, mode_count)
    forward_table = table[:, :lon_local].astype(jnp.bfloat16)
    inverse_table = table.astype(jnp.bfloat16)
    outgoing = courant.transpose(0, 2, 1, 3).astype(jnp.bfloat16)
    outgoing = outgoing.reshape(blocks, (2 * row_count // blocks) * lon_local, levels)
    pair_factor = jnp.repeat(1.0 - row_factor, 2, axis=0)
    removal = jnp.concatenate([pair_factor, pair_factor], axis=1) * mode_weight[None, :]
    arrived = lax.all_to_all(outgoing, "lon", split_axis=0, concat_axis=0, tiled=True)
    level_block = arrived.reshape(blocks, per_device // 2, lon_local, 2, levels)
    first_row = lax.axis_index("lon") * per_device
    local_removal = lax.dynamic_slice_in_dim(removal, first_row, per_device, 0)
    spectrum = jnp.einsum(
        "drjcl,djm->rcml", level_block, forward_table, preferred_element_type=jnp.float32
    ).reshape(per_device, 2 * mode_count, levels)
    weighted = (spectrum * local_removal[:, :, None]).astype(jnp.bfloat16)
    correction = jnp.einsum(
        "rcml,djm->drjcl",
        weighted.reshape(per_device // 2, 2, 2 * mode_count, levels),
        inverse_table,
        preferred_element_type=jnp.float32,
    ).astype(jnp.bfloat16)
    correction = correction.reshape(blocks, per_device * (lon_local + 1), levels)
    returned = lax.all_to_all(correction, "lon", split_axis=0, concat_axis=0, tiled=True)
    return returned.reshape(row_count, lon_local + 1, 2, levels)


def local(tracers, courant, row_mask, damped_modes, damping):
    rows_local = courant.shape[0]
    lon_local = courant.shape[2]
    mode_count = damping.shape[1]
    tracer_count = tracers.shape[0]
    lon_size = lax.axis_size("lon")
    mode_index = jnp.arange(mode_count, dtype=jnp.int32)
    damped = (row_mask[:, None] == 1) & (mode_index[None, :] >= mode_count - damped_modes[:, None])
    factor = jnp.where(damped, damping, 1.0)
    tracer_wide = padded(tracers, (("lon", 2),), 3, True).astype(jnp.float32)
    east_column = lax.ppermute(
        courant[:, 0, 0:1], "lon", [(i, (i - 1) % lon_size) for i in range(lon_size)]
    )
    correction = filter_correction(courant, factor).astype(jnp.float32)
    zonal_courant = jnp.concatenate([courant[:, 0], east_column], axis=1)
    zonal_faces = (zonal_courant - correction[:, :, 0]).astype(jnp.bfloat16)
    meridional_filtered = (courant[:, 1] - correction[:, :lon_local, 1]).astype(jnp.bfloat16)
    middle = (
        tracers.astype(jnp.float32)
        + ppm_change(tracer_wide, zonal_faces.astype(jnp.float32)[None], 2, lon_local)
    ).astype(jnp.bfloat16)
    meridional_stack = jnp.concatenate([middle, meridional_filtered[None]], axis=0)
    meridional_band = padded(meridional_stack, (("lat", 1),), 3, False)
    middle_wide = meridional_band[:tracer_count].astype(jnp.float32)
    meridional_faces = meridional_band[tracer_count, 3 : rows_local + 4].astype(jnp.float32)
    face_rows = lax.axis_index("lat") * rows_local + jnp.arange(rows_local + 1, dtype=jnp.int32)
    meridional_faces = jnp.where(face_rows[:, None, None] > 0, meridional_faces, 0.0)
    return (
        middle.astype(jnp.float32) + ppm_change(middle_wide, meridional_faces[None], 1, rows_local)
    ).astype(jnp.bfloat16)


def solution(mesh):
    placed = (
        P(None, "lat", "lon", None),
        P("lat", None, "lon", None),
        P("lat"),
        P("lat"),
        P("lat", None),
    )
    return jax.shard_map(
        local, mesh=mesh, in_specs=placed, out_specs=P(None, "lat", "lon", None), check_vma=False
    )
```

```python
import math

import jax
import jax.numpy as jnp
from jax import lax
from jax.sharding import PartitionSpec as P


def padded(value, sides, width, wrap):
    for axis, dim in sides:
        size, length = (lax.axis_size(axis), value.shape[dim])
        up = [(i, (i + 1) % size) for i in range(size if wrap else size - 1)]
        down = [(j, i) for i, j in up]
        last = lax.slice_in_dim(value, length - width, length, axis=dim)
        leading = lax.slice_in_dim(value, 0, width, axis=dim)
        before = lax.ppermute(last, axis, up)
        after = lax.ppermute(leading, axis, down)
        value = jnp.concatenate([before, value, after], axis=dim)
    return value


def take_slice(values, low_end, high_end, along_axis):
    return lax.slice_in_dim(values, low_end, high_end, axis=along_axis)


def ppm_change(extended, courant_faces, along_axis, count_cells):
    edge_values = 7.0 / 12.0 * (
        take_slice(extended, 1, count_cells + 4, along_axis)
        + take_slice(extended, 2, count_cells + 5, along_axis)
    ) - 1.0 / 12.0 * (
        take_slice(extended, 0, count_cells + 3, along_axis)
        + take_slice(extended, 3, count_cells + 6, along_axis)
    )
    left_edge = take_slice(edge_values, 0, count_cells + 2, along_axis)
    right_edge = take_slice(edge_values, 1, count_cells + 3, along_axis)
    centre = take_slice(extended, 2, count_cells + 4, along_axis)
    slope_edge = right_edge - left_edge
    curvature = 6.0 * (centre - 0.5 * (left_edge + right_edge))
    upwind_plus = courant_faces * (
        take_slice(right_edge, 0, count_cells + 1, along_axis)
        - 0.5
        * courant_faces
        * (
            take_slice(slope_edge, 0, count_cells + 1, along_axis)
            - (1.0 - courant_faces * (2.0 / 3.0))
            * take_slice(curvature, 0, count_cells + 1, along_axis)
        )
    )
    upwind_minus = courant_faces * (
        take_slice(left_edge, 1, count_cells + 2, along_axis)
        - 0.5
        * courant_faces
        * (
            take_slice(slope_edge, 1, count_cells + 2, along_axis)
            + (1.0 + courant_faces * (2.0 / 3.0))
            * take_slice(curvature, 1, count_cells + 2, along_axis)
        )
    )
    face_flux = jnp.where(courant_faces > 0, upwind_plus, upwind_minus)
    return take_slice(face_flux, 0, count_cells, along_axis) - take_slice(
        face_flux, 1, count_cells + 1, along_axis
    )


def spectral_basis(blocks, block_len, span, mode_count):
    total_lon = blocks * block_len
    scale = 2.0 * math.pi / total_lon
    mode_index = jnp.arange(mode_count, dtype=jnp.int32)[None, :]
    coarse = jnp.arange(blocks, dtype=jnp.int32)[:, None]
    fine = jnp.arange(span, dtype=jnp.int32)[:, None]
    coarse_angle = ((block_len * coarse * mode_index) % total_lon).astype(jnp.float32) * scale
    fine_angle = ((fine * mode_index) % total_lon).astype(jnp.float32) * scale
    cc, sc = jnp.cos(coarse_angle)[:, None, :], jnp.sin(coarse_angle)[:, None, :]
    cf, sf = jnp.cos(fine_angle)[None], jnp.sin(fine_angle)[None]
    cosine = cc * cf - sc * sf
    sine = sc * cf + cc * sf
    table = jnp.concatenate([cosine, -sine], axis=2)
    mode_weight = (
        jnp.where((mode_index[0] == 0) | (2 * mode_index[0] == total_lon), 1.0, 2.0) / total_lon
    )
    return table, jnp.concatenate([mode_weight, mode_weight], axis=0)


def filter_correction(courant, row_factor):
    row_count, _, lon_local, levels = courant.shape
    blocks = lax.axis_size("lon")
    mode_count = row_factor.shape[1]
    per_device = 2 * row_count // blocks
    rows_here = per_device // 2
    table, mode_weight = spectral_basis(blocks, lon_local, lon_local + 1, mode_count)
    forward_table = table[:, :lon_local].reshape(blocks * lon_local, 2 * mode_count)
    inverse_table = table.reshape(blocks * (lon_local + 1), 2 * mode_count).astype(jnp.bfloat16)
    outgoing = courant.transpose(0, 2, 1, 3).reshape(row_count, lon_local, 2 * levels)
    outgoing = outgoing.astype(jnp.bfloat16).reshape(blocks, rows_here * lon_local, 2 * levels)
    pair_factor = jnp.repeat(1.0 - row_factor, 2, axis=0)
    removal = jnp.concatenate([pair_factor, pair_factor], axis=1) * mode_weight[None, :]
    arrived = lax.all_to_all(outgoing, "lon", split_axis=0, concat_axis=0, tiled=True)
    first_row = lax.axis_index("lon") * per_device
    local_removal = lax.dynamic_slice_in_dim(removal, first_row, per_device, 0)
    local_removal = local_removal.reshape(rows_here, 2, 2 * mode_count).transpose(0, 2, 1)
    gathered = arrived.reshape(blocks, rows_here, lon_local, 2 * levels)
    spectrum = jnp.einsum(
        "drjk,djm->rmk",
        gathered,
        forward_table.astype(jnp.bfloat16).reshape(blocks, lon_local, 2 * mode_count),
        preferred_element_type=jnp.float32,
    ).reshape(rows_here, 2 * mode_count, 2, levels)
    weighted = (spectrum * local_removal[:, :, :, None]).astype(jnp.bfloat16)
    correction = jnp.einsum(
        "rmk,pm->prk",
        weighted.reshape(rows_here, 2 * mode_count, 2 * levels),
        inverse_table,
        preferred_element_type=jnp.float32,
    ).astype(jnp.bfloat16)
    correction = correction.reshape(blocks, lon_local + 1, rows_here, 2 * levels)
    correction = correction.transpose(0, 2, 1, 3).reshape(blocks, rows_here * (lon_local + 1), 2 * levels)
    returned = lax.all_to_all(correction, "lon", split_axis=0, concat_axis=0, tiled=True)
    return returned.reshape(row_count, lon_local + 1, 2, levels)


def local(tracers, courant, row_mask, damped_modes, damping):
    rows_local = courant.shape[0]
    lon_local = courant.shape[2]
    mode_count = damping.shape[1]
    tracer_count = tracers.shape[0]
    lon_size = lax.axis_size("lon")
    mode_index = jnp.arange(mode_count, dtype=jnp.int32)
    damped = (row_mask[:, None] == 1) & (mode_index[None, :] >= mode_count - damped_modes[:, None])
    factor = jnp.where(damped, damping, 1.0)
    tracer_wide = padded(tracers, (("lon", 2),), 3, True).astype(jnp.float32)
    east_column = lax.ppermute(
        courant[:, 0, 0:1], "lon", [(i, (i - 1) % lon_size) for i in range(lon_size)]
    )
    correction = filter_correction(courant, factor).astype(jnp.float32)
    zonal_courant = jnp.concatenate([courant[:, 0], east_column], axis=1)
    zonal_faces = (zonal_courant - correction[:, :, 0]).astype(jnp.bfloat16)
    meridional_filtered = (courant[:, 1] - correction[:, :lon_local, 1]).astype(jnp.bfloat16)
    middle = (
        tracers.astype(jnp.float32)
        + ppm_change(tracer_wide, zonal_faces.astype(jnp.float32)[None], 2, lon_local)
    ).astype(jnp.bfloat16)
    meridional_stack = jnp.concatenate([middle, meridional_filtered[None]], axis=0)
    meridional_band = padded(meridional_stack, (("lat", 1),), 3, False)
    middle_wide = meridional_band[:tracer_count].astype(jnp.float32)
    meridional_faces = meridional_band[tracer_count, 3 : rows_local + 4].astype(jnp.float32)
    face_rows = lax.axis_index("lat") * rows_local + jnp.arange(rows_local + 1, dtype=jnp.int32)
    meridional_faces = jnp.where(face_rows[:, None, None] > 0, meridional_faces, 0.0)
    return (
        middle.astype(jnp.float32) + ppm_change(middle_wide, meridional_faces[None], 1, rows_local)
    ).astype(jnp.bfloat16)


def solution(mesh):
    placed = (
        P(None, "lat", "lon", None),
        P("lat", None, "lon", None),
        P("lat"),
        P("lat"),
        P("lat", None),
    )
    return jax.shard_map(
        local, mesh=mesh, in_specs=placed, out_specs=P(None, "lat", "lon", None), check_vma=False
    )
```

```python
import math

import jax
import jax.numpy as jnp
from jax import lax
from jax.sharding import PartitionSpec as P


def padded(value, sides, width, wrap):
    for axis, dim in sides:
        size, length = (lax.axis_size(axis), value.shape[dim])
        up = [(i, (i + 1) % size) for i in range(size if wrap else size - 1)]
        down = [(j, i) for i, j in up]
        last = lax.slice_in_dim(value, length - width, length, axis=dim)
        leading = lax.slice_in_dim(value, 0, width, axis=dim)
        before = lax.ppermute(last, axis, up)
        after = lax.ppermute(leading, axis, down)
        value = jnp.concatenate([before, value, after], axis=dim)
    return value


def take_slice(values, low_end, high_end, along_axis):
    return lax.slice_in_dim(values, low_end, high_end, axis=along_axis)


def ppm_change(extended, courant_faces, along_axis, count_cells):
    edge_values = 7.0 / 12.0 * (
        take_slice(extended, 1, count_cells + 4, along_axis)
        + take_slice(extended, 2, count_cells + 5, along_axis)
    ) - 1.0 / 12.0 * (
        take_slice(extended, 0, count_cells + 3, along_axis)
        + take_slice(extended, 3, count_cells + 6, along_axis)
    )
    left_edge = take_slice(edge_values, 0, count_cells + 2, along_axis)
    right_edge = take_slice(edge_values, 1, count_cells + 3, along_axis)
    centre = take_slice(extended, 2, count_cells + 4, along_axis)
    slope_edge = right_edge - left_edge
    curvature = 6.0 * (centre - 0.5 * (left_edge + right_edge))
    upwind_plus = courant_faces * (
        take_slice(right_edge, 0, count_cells + 1, along_axis)
        - 0.5
        * courant_faces
        * (
            take_slice(slope_edge, 0, count_cells + 1, along_axis)
            - (1.0 - courant_faces * (2.0 / 3.0))
            * take_slice(curvature, 0, count_cells + 1, along_axis)
        )
    )
    upwind_minus = courant_faces * (
        take_slice(left_edge, 1, count_cells + 2, along_axis)
        - 0.5
        * courant_faces
        * (
            take_slice(slope_edge, 1, count_cells + 2, along_axis)
            + (1.0 + courant_faces * (2.0 / 3.0))
            * take_slice(curvature, 1, count_cells + 2, along_axis)
        )
    )
    face_flux = jnp.where(courant_faces > 0, upwind_plus, upwind_minus)
    return take_slice(face_flux, 0, count_cells, along_axis) - take_slice(
        face_flux, 1, count_cells + 1, along_axis
    )


def spectral_basis(blocks, block_len, span, mode_count):
    total_lon = blocks * block_len
    scale = 2.0 * math.pi / total_lon
    mode_index = jnp.arange(mode_count, dtype=jnp.int32)[None, :]
    coarse = jnp.arange(blocks, dtype=jnp.int32)[:, None]
    fine = jnp.arange(span, dtype=jnp.int32)[:, None]
    coarse_angle = ((block_len * coarse * mode_index) % total_lon).astype(jnp.float32) * scale
    fine_angle = ((fine * mode_index) % total_lon).astype(jnp.float32) * scale
    cc, sc = jnp.cos(coarse_angle)[:, None, :], jnp.sin(coarse_angle)[:, None, :]
    cf, sf = jnp.cos(fine_angle)[None], jnp.sin(fine_angle)[None]
    cosine = cc * cf - sc * sf
    sine = sc * cf + cc * sf
    table = jnp.concatenate([cosine, -sine], axis=2)
    mode_weight = (
        jnp.where((mode_index[0] == 0) | (2 * mode_index[0] == total_lon), 1.0, 2.0) / total_lon
    )
    return table, jnp.concatenate([mode_weight, mode_weight], axis=0)


def filter_correction(courant, row_factor):
    row_count, _, lon_local, levels = courant.shape
    blocks = lax.axis_size("lon")
    mode_count = row_factor.shape[1]
    per_device = 2 * row_count // blocks
    table, mode_weight = spectral_basis(blocks, lon_local, lon_local + 1, mode_count)
    forward_table = table[:, :lon_local].astype(jnp.bfloat16)
    inverse_table = table.astype(jnp.bfloat16)
    outgoing = courant.transpose(0, 2, 1, 3).astype(jnp.bfloat16)
    outgoing = outgoing.reshape(blocks, (2 * row_count // blocks) * lon_local, levels)
    pair_factor = jnp.repeat(1.0 - row_factor, 2, axis=0)
    removal = jnp.concatenate([pair_factor, pair_factor], axis=1) * mode_weight[None, :]
    arrived = lax.all_to_all(outgoing, "lon", split_axis=0, concat_axis=0, tiled=True)
    level_block = arrived.reshape(blocks, per_device // 2, lon_local, 2, levels)
    first_row = lax.axis_index("lon") * per_device
    local_removal = lax.dynamic_slice_in_dim(removal, first_row, per_device, 0)
    spectrum = jnp.einsum(
        "mdj,drjcl->mrcl",
        forward_table.transpose(2, 0, 1),
        level_block,
        preferred_element_type=jnp.float32,
    )
    pair_removal = local_removal.reshape(per_device // 2, 2, 2 * mode_count).transpose(2, 0, 1)
    weighted = (spectrum * pair_removal[:, :, :, None]).astype(jnp.bfloat16)
    correction = jnp.einsum(
        "pm,mrcl->prcl",
        inverse_table.reshape(blocks * (lon_local + 1), 2 * mode_count),
        weighted,
        preferred_element_type=jnp.float32,
    ).astype(jnp.bfloat16)
    correction = correction.reshape(blocks, lon_local + 1, per_device // 2, 2, levels)
    correction = correction.transpose(0, 2, 1, 3, 4)
    correction = correction.reshape(blocks, per_device * (lon_local + 1), levels)
    returned = lax.all_to_all(correction, "lon", split_axis=0, concat_axis=0, tiled=True)
    return returned.reshape(row_count, lon_local + 1, 2, levels)


def local(tracers, courant, row_mask, damped_modes, damping):
    rows_local = courant.shape[0]
    lon_local = courant.shape[2]
    mode_count = damping.shape[1]
    tracer_count = tracers.shape[0]
    lon_size = lax.axis_size("lon")
    mode_index = jnp.arange(mode_count, dtype=jnp.int32)
    damped = (row_mask[:, None] == 1) & (mode_index[None, :] >= mode_count - damped_modes[:, None])
    factor = jnp.where(damped, damping, 1.0)
    tracer_wide = padded(tracers, (("lon", 2),), 3, True).astype(jnp.float32)
    east_column = lax.ppermute(
        courant[:, 0, 0:1], "lon", [(i, (i - 1) % lon_size) for i in range(lon_size)]
    )
    correction = filter_correction(courant, factor).astype(jnp.float32)
    zonal_courant = jnp.concatenate([courant[:, 0], east_column], axis=1)
    zonal_faces = (zonal_courant - correction[:, :, 0]).astype(jnp.bfloat16)
    meridional_filtered = (courant[:, 1] - correction[:, :lon_local, 1]).astype(jnp.bfloat16)
    def zonal_step(low, high):
        return (
            tracers[:, low:high].astype(jnp.float32)
            + ppm_change(
                tracer_wide[:, low:high],
                zonal_faces[low:high].astype(jnp.float32)[None],
                2,
                lon_local,
            )
        ).astype(jnp.bfloat16)

    lat_size = lax.axis_size("lat")
    southward = jnp.concatenate(
        [zonal_step(0, 3), meridional_filtered[None, 0:1]], axis=1
    )
    northward = zonal_step(rows_local - 3, rows_local)
    from_north = lax.ppermute(southward, "lat", [(i, i - 1) for i in range(1, lat_size)])
    from_south = lax.ppermute(northward, "lat", [(i, i + 1) for i in range(lat_size - 1)])
    middle = zonal_step(0, rows_local)
    middle_wide = jnp.concatenate([from_south, middle, from_north[:, 0:3]], axis=1)
    middle_wide = middle_wide.astype(jnp.float32)
    meridional_faces = jnp.concatenate(
        [meridional_filtered, from_north[0, 3:4]], axis=0
    ).astype(jnp.float32)
    face_rows = lax.axis_index("lat") * rows_local + jnp.arange(rows_local + 1, dtype=jnp.int32)
    meridional_faces = jnp.where(face_rows[:, None, None] > 0, meridional_faces, 0.0)
    return (
        middle.astype(jnp.float32) + ppm_change(middle_wide, meridional_faces[None], 1, rows_local)
    ).astype(jnp.bfloat16)


def solution(mesh):
    placed = (
        P(None, "lat", "lon", None),
        P("lat", None, "lon", None),
        P("lat"),
        P("lat"),
        P("lat", None),
    )
    return jax.shard_map(
        local, mesh=mesh, in_specs=placed, out_specs=P(None, "lat", "lon", None), check_vma=False
    )
```

```python
import math

import jax
import jax.numpy as jnp
from jax import lax
from jax.sharding import PartitionSpec as P


def padded(value, sides, width, wrap):
    for axis, dim in sides:
        size, length = (lax.axis_size(axis), value.shape[dim])
        up = [(i, (i + 1) % size) for i in range(size if wrap else size - 1)]
        down = [(j, i) for i, j in up]
        last = lax.slice_in_dim(value, length - width, length, axis=dim)
        leading = lax.slice_in_dim(value, 0, width, axis=dim)
        before = lax.ppermute(last, axis, up)
        after = lax.ppermute(leading, axis, down)
        value = jnp.concatenate([before, value, after], axis=dim)
    return value


def take_slice(values, low_end, high_end, along_axis):
    return lax.slice_in_dim(values, low_end, high_end, axis=along_axis)


def ppm_change(extended, courant_faces, along_axis, count_cells):
    edge_values = 7.0 / 12.0 * (
        take_slice(extended, 1, count_cells + 4, along_axis)
        + take_slice(extended, 2, count_cells + 5, along_axis)
    ) - 1.0 / 12.0 * (
        take_slice(extended, 0, count_cells + 3, along_axis)
        + take_slice(extended, 3, count_cells + 6, along_axis)
    )
    left_edge = take_slice(edge_values, 0, count_cells + 2, along_axis)
    right_edge = take_slice(edge_values, 1, count_cells + 3, along_axis)
    centre = take_slice(extended, 2, count_cells + 4, along_axis)
    slope_edge = right_edge - left_edge
    curvature = 6.0 * (centre - 0.5 * (left_edge + right_edge))
    upwind_plus = courant_faces * (
        take_slice(right_edge, 0, count_cells + 1, along_axis)
        - 0.5
        * courant_faces
        * (
            take_slice(slope_edge, 0, count_cells + 1, along_axis)
            - (1.0 - courant_faces * (2.0 / 3.0))
            * take_slice(curvature, 0, count_cells + 1, along_axis)
        )
    )
    upwind_minus = courant_faces * (
        take_slice(left_edge, 1, count_cells + 2, along_axis)
        - 0.5
        * courant_faces
        * (
            take_slice(slope_edge, 1, count_cells + 2, along_axis)
            + (1.0 + courant_faces * (2.0 / 3.0))
            * take_slice(curvature, 1, count_cells + 2, along_axis)
        )
    )
    face_flux = jnp.where(courant_faces > 0, upwind_plus, upwind_minus)
    return take_slice(face_flux, 0, count_cells, along_axis) - take_slice(
        face_flux, 1, count_cells + 1, along_axis
    )


def spectral_basis(blocks, block_len, span, mode_count):
    total_lon = blocks * block_len
    scale = 2.0 * math.pi / total_lon
    mode_index = jnp.arange(mode_count, dtype=jnp.int32)[None, :]
    coarse = jnp.arange(blocks, dtype=jnp.int32)[:, None]
    fine = jnp.arange(span, dtype=jnp.int32)[:, None]
    coarse_angle = ((block_len * coarse * mode_index) % total_lon).astype(jnp.float32) * scale
    fine_angle = ((fine * mode_index) % total_lon).astype(jnp.float32) * scale
    cc, sc = jnp.cos(coarse_angle)[:, None, :], jnp.sin(coarse_angle)[:, None, :]
    cf, sf = jnp.cos(fine_angle)[None], jnp.sin(fine_angle)[None]
    cosine = cc * cf - sc * sf
    sine = sc * cf + cc * sf
    table = jnp.concatenate([cosine, -sine], axis=2)
    mode_weight = (
        jnp.where((mode_index[0] == 0) | (2 * mode_index[0] == total_lon), 1.0, 2.0) / total_lon
    )
    return table, jnp.concatenate([mode_weight, mode_weight], axis=0)


def filter_correction(courant, row_factor):
    row_count, _, lon_local, levels = courant.shape
    blocks = lax.axis_size("lon")
    mode_count = row_factor.shape[1]
    per_device = 2 * row_count // blocks
    table, mode_weight = spectral_basis(blocks, lon_local, lon_local + 1, mode_count)
    forward_table = table[:, :lon_local].astype(jnp.bfloat16)
    inverse_table = table.astype(jnp.bfloat16)
    outgoing = courant.transpose(0, 2, 1, 3).astype(jnp.bfloat16)
    outgoing = outgoing.reshape(blocks, (2 * row_count // blocks) * lon_local, levels)
    pair_factor = jnp.repeat(1.0 - row_factor, 2, axis=0)
    removal = jnp.concatenate([pair_factor, pair_factor], axis=1) * mode_weight[None, :]
    arrived = lax.all_to_all(outgoing, "lon", split_axis=0, concat_axis=0, tiled=True)
    level_block = arrived.reshape(blocks, per_device // 2, lon_local, 2, levels)
    first_row = lax.axis_index("lon") * per_device
    local_removal = lax.dynamic_slice_in_dim(removal, first_row, per_device, 0)
    spectrum = jnp.einsum(
        "drjcl,djm->rcml", level_block, forward_table, preferred_element_type=jnp.float32
    ).reshape(per_device, 2 * mode_count, levels)
    weighted = (spectrum * local_removal[:, :, None]).astype(jnp.bfloat16)
    correction = jnp.einsum(
        "rcml,djm->drjcl",
        weighted.reshape(per_device // 2, 2, 2 * mode_count, levels),
        inverse_table,
        preferred_element_type=jnp.float32,
    ).astype(jnp.bfloat16)
    correction = correction.reshape(blocks, per_device * (lon_local + 1), levels)
    returned = lax.all_to_all(correction, "lon", split_axis=0, concat_axis=0, tiled=True)
    return returned.reshape(row_count, lon_local + 1, 2, levels)


def local(tracers, courant, row_mask, damped_modes, damping):
    rows_local = courant.shape[0]
    lon_local = courant.shape[2]
    mode_count = damping.shape[1]
    tracer_count = tracers.shape[0]
    lon_size = lax.axis_size("lon")
    mode_index = jnp.arange(mode_count, dtype=jnp.int32)
    damped = (row_mask[:, None] == 1) & (mode_index[None, :] >= mode_count - damped_modes[:, None])
    factor = jnp.where(damped, damping, 1.0)
    tracer_wide = padded(tracers, (("lon", 2),), 3, True).astype(jnp.float32)
    east_column = lax.ppermute(
        courant[:, 0, 0:1], "lon", [(i, (i - 1) % lon_size) for i in range(lon_size)]
    )
    correction = filter_correction(courant, factor).astype(jnp.float32)
    zonal_courant = jnp.concatenate([courant[:, 0], east_column], axis=1)
    zonal_faces = (zonal_courant - correction[:, :, 0]).astype(jnp.bfloat16)
    meridional_filtered = (courant[:, 1] - correction[:, :lon_local, 1]).astype(jnp.bfloat16)
    def zonal_step(low, high):
        return (
            tracers[:, low:high].astype(jnp.float32)
            + ppm_change(
                tracer_wide[:, low:high],
                zonal_faces[low:high].astype(jnp.float32)[None],
                2,
                lon_local,
            )
        ).astype(jnp.bfloat16)

    lat_size = lax.axis_size("lat")
    southward = jnp.concatenate(
        [zonal_step(0, 3), meridional_filtered[None, 0:1]], axis=1
    )
    northward = zonal_step(rows_local - 3, rows_local)
    from_north = lax.ppermute(southward, "lat", [(i, i - 1) for i in range(1, lat_size)])
    from_south = lax.ppermute(northward, "lat", [(i, i + 1) for i in range(lat_size - 1)])
    middle = zonal_step(0, rows_local)
    middle_wide = jnp.concatenate([from_south, middle, from_north[:, 0:3]], axis=1)
    middle_wide = middle_wide.astype(jnp.float32)
    meridional_faces = jnp.concatenate(
        [meridional_filtered, from_north[0, 3:4]], axis=0
    ).astype(jnp.float32)
    face_rows = lax.axis_index("lat") * rows_local + jnp.arange(rows_local + 1, dtype=jnp.int32)
    meridional_faces = jnp.where(face_rows[:, None, None] > 0, meridional_faces, 0.0)
    return (
        middle.astype(jnp.float32) + ppm_change(middle_wide, meridional_faces[None], 1, rows_local)
    ).astype(jnp.bfloat16)


def solution(mesh):
    placed = (
        P(None, "lat", "lon", None),
        P("lat", None, "lon", None),
        P("lat"),
        P("lat"),
        P("lat", None),
    )
    return jax.shard_map(
        local, mesh=mesh, in_specs=placed, out_specs=P(None, "lat", "lon", None), check_vma=False
    )
```

```python
import math

import jax
import jax.numpy as jnp
from jax import lax
from jax.sharding import PartitionSpec as P


def padded(value, sides, width, wrap):
    for axis, dim in sides:
        size, length = (lax.axis_size(axis), value.shape[dim])
        up = [(i, (i + 1) % size) for i in range(size if wrap else size - 1)]
        down = [(j, i) for i, j in up]
        last = lax.slice_in_dim(value, length - width, length, axis=dim)
        leading = lax.slice_in_dim(value, 0, width, axis=dim)
        before = lax.ppermute(last, axis, up)
        after = lax.ppermute(leading, axis, down)
        value = jnp.concatenate([before, value, after], axis=dim)
    return value


def take_slice(values, low_end, high_end, along_axis):
    return lax.slice_in_dim(values, low_end, high_end, axis=along_axis)


def ppm_change(extended, courant_faces, along_axis, count_cells):
    edge_values = 7.0 / 12.0 * (
        take_slice(extended, 1, count_cells + 4, along_axis)
        + take_slice(extended, 2, count_cells + 5, along_axis)
    ) - 1.0 / 12.0 * (
        take_slice(extended, 0, count_cells + 3, along_axis)
        + take_slice(extended, 3, count_cells + 6, along_axis)
    )
    left_edge = take_slice(edge_values, 0, count_cells + 2, along_axis)
    right_edge = take_slice(edge_values, 1, count_cells + 3, along_axis)
    centre = take_slice(extended, 2, count_cells + 4, along_axis)
    slope_edge = right_edge - left_edge
    curvature = 6.0 * (centre - 0.5 * (left_edge + right_edge))
    upwind_plus = courant_faces * (
        take_slice(right_edge, 0, count_cells + 1, along_axis)
        - 0.5
        * courant_faces
        * (
            take_slice(slope_edge, 0, count_cells + 1, along_axis)
            - (1.0 - courant_faces * (2.0 / 3.0))
            * take_slice(curvature, 0, count_cells + 1, along_axis)
        )
    )
    upwind_minus = courant_faces * (
        take_slice(left_edge, 1, count_cells + 2, along_axis)
        - 0.5
        * courant_faces
        * (
            take_slice(slope_edge, 1, count_cells + 2, along_axis)
            + (1.0 + courant_faces * (2.0 / 3.0))
            * take_slice(curvature, 1, count_cells + 2, along_axis)
        )
    )
    face_flux = jnp.where(courant_faces > 0, upwind_plus, upwind_minus)
    return take_slice(face_flux, 0, count_cells, along_axis) - take_slice(
        face_flux, 1, count_cells + 1, along_axis
    )


def spectral_basis(blocks, block_len, span, mode_count):
    total_lon = blocks * block_len
    scale = 2.0 * math.pi / total_lon
    mode_index = jnp.arange(mode_count, dtype=jnp.int32)[None, :]
    coarse = jnp.arange(blocks, dtype=jnp.int32)[:, None]
    fine = jnp.arange(span, dtype=jnp.int32)[:, None]
    coarse_angle = ((block_len * coarse * mode_index) % total_lon).astype(jnp.float32) * scale
    fine_angle = ((fine * mode_index) % total_lon).astype(jnp.float32) * scale
    cc, sc = jnp.cos(coarse_angle)[:, None, :], jnp.sin(coarse_angle)[:, None, :]
    cf, sf = jnp.cos(fine_angle)[None], jnp.sin(fine_angle)[None]
    cosine = cc * cf - sc * sf
    sine = sc * cf + cc * sf
    table = jnp.concatenate([cosine, -sine], axis=2)
    mode_weight = (
        jnp.where((mode_index[0] == 0) | (2 * mode_index[0] == total_lon), 1.0, 2.0) / total_lon
    )
    return table, jnp.concatenate([mode_weight, mode_weight], axis=0)


def filter_correction(courant, row_factor):
    row_count, _, lon_local, levels = courant.shape
    blocks = lax.axis_size("lon")
    mode_count = row_factor.shape[1]
    per_device = 2 * row_count // blocks
    table, mode_weight = spectral_basis(blocks, lon_local, lon_local + 1, mode_count)
    forward_table = spectral_basis(blocks, lon_local, lon_local, mode_count)[0].astype(jnp.bfloat16)
    inverse_table = table.astype(jnp.bfloat16)
    outgoing = courant.transpose(0, 2, 1, 3).astype(jnp.bfloat16)
    outgoing = outgoing.reshape(blocks, (2 * row_count // blocks) * lon_local, levels)
    pair_factor = jnp.repeat(1.0 - row_factor, 2, axis=0)
    removal = jnp.concatenate([pair_factor, pair_factor], axis=1) * mode_weight[None, :]
    arrived = lax.all_to_all(outgoing, "lon", split_axis=0, concat_axis=0, tiled=True)
    level_block = arrived.reshape(blocks, per_device // 2, lon_local, 2, levels)
    first_row = lax.axis_index("lon") * per_device
    local_removal = lax.dynamic_slice_in_dim(removal, first_row, per_device, 0)
    spectrum = jnp.einsum(
        "drjcl,djm->rcml", level_block, forward_table, preferred_element_type=jnp.float32
    ).reshape(per_device, 2 * mode_count, levels)
    weighted = lax.optimization_barrier((spectrum * local_removal[:, :, None]).astype(jnp.bfloat16))
    correction = jnp.einsum(
        "rcml,djm->drjcl",
        weighted.reshape(per_device // 2, 2, 2 * mode_count, levels),
        inverse_table,
        preferred_element_type=jnp.float32,
    ).astype(jnp.bfloat16)
    correction = correction.reshape(blocks, per_device * (lon_local + 1), levels)
    returned = lax.all_to_all(correction, "lon", split_axis=0, concat_axis=0, tiled=True)
    return returned.reshape(row_count, lon_local + 1, 2, levels)


def local(tracers, courant, row_mask, damped_modes, damping):
    rows_local = courant.shape[0]
    lon_local = courant.shape[2]
    mode_count = damping.shape[1]
    tracer_count = tracers.shape[0]
    lon_size = lax.axis_size("lon")
    mode_index = jnp.arange(mode_count, dtype=jnp.int32)
    damped = (row_mask[:, None] == 1) & (mode_index[None, :] >= mode_count - damped_modes[:, None])
    factor = jnp.where(damped, damping, 1.0)
    tracer_wide = padded(tracers, (("lon", 2),), 3, True).astype(jnp.float32)
    east_column = lax.ppermute(
        courant[:, 0, 0:1], "lon", [(i, (i - 1) % lon_size) for i in range(lon_size)]
    )
    correction = filter_correction(courant, factor).astype(jnp.float32)
    zonal_courant = jnp.concatenate([courant[:, 0], east_column], axis=1)
    zonal_faces = (zonal_courant - correction[:, :, 0]).astype(jnp.bfloat16)
    meridional_filtered = (courant[:, 1] - correction[:, :lon_local, 1]).astype(jnp.bfloat16)
    middle = (
        tracers.astype(jnp.float32)
        + ppm_change(tracer_wide, zonal_faces.astype(jnp.float32)[None], 2, lon_local)
    ).astype(jnp.bfloat16)
    meridional_stack = jnp.concatenate([middle, meridional_filtered[None]], axis=0)
    meridional_band = padded(meridional_stack, (("lat", 1),), 3, False)
    middle_wide = meridional_band[:tracer_count].astype(jnp.float32)
    meridional_faces = meridional_band[tracer_count, 3 : rows_local + 4].astype(jnp.float32)
    face_rows = lax.axis_index("lat") * rows_local + jnp.arange(rows_local + 1, dtype=jnp.int32)
    meridional_faces = jnp.where(face_rows[:, None, None] > 0, meridional_faces, 0.0)
    return (
        middle.astype(jnp.float32) + ppm_change(middle_wide, meridional_faces[None], 1, rows_local)
    ).astype(jnp.bfloat16)


def solution(mesh):
    placed = (
        P(None, "lat", "lon", None),
        P("lat", None, "lon", None),
        P("lat"),
        P("lat"),
        P("lat", None),
    )
    return jax.shard_map(
        local, mesh=mesh, in_specs=placed, out_specs=P(None, "lat", "lon", None), check_vma=False
    )
```

```python
import math

import jax
import jax.numpy as jnp
from jax import lax
from jax.sharding import PartitionSpec as P


def padded(value, sides, width, wrap):
    for axis, dim in sides:
        size, length = (lax.axis_size(axis), value.shape[dim])
        up = [(i, (i + 1) % size) for i in range(size if wrap else size - 1)]
        down = [(j, i) for i, j in up]
        last = lax.slice_in_dim(value, length - width, length, axis=dim)
        leading = lax.slice_in_dim(value, 0, width, axis=dim)
        before = lax.ppermute(last, axis, up)
        after = lax.ppermute(leading, axis, down)
        value = jnp.concatenate([before, value, after], axis=dim)
    return value


def take_slice(values, low_end, high_end, along_axis):
    return lax.slice_in_dim(values, low_end, high_end, axis=along_axis)


def ppm_change(extended, courant_faces, along_axis, count_cells):
    edge_values = 7.0 / 12.0 * (
        take_slice(extended, 1, count_cells + 4, along_axis)
        + take_slice(extended, 2, count_cells + 5, along_axis)
    ) - 1.0 / 12.0 * (
        take_slice(extended, 0, count_cells + 3, along_axis)
        + take_slice(extended, 3, count_cells + 6, along_axis)
    )
    left_edge = take_slice(edge_values, 0, count_cells + 2, along_axis)
    right_edge = take_slice(edge_values, 1, count_cells + 3, along_axis)
    centre = take_slice(extended, 2, count_cells + 4, along_axis)
    slope_edge = right_edge - left_edge
    curvature = 6.0 * (centre - 0.5 * (left_edge + right_edge))
    upwind_plus = courant_faces * (
        take_slice(right_edge, 0, count_cells + 1, along_axis)
        - 0.5
        * courant_faces
        * (
            take_slice(slope_edge, 0, count_cells + 1, along_axis)
            - (1.0 - courant_faces * (2.0 / 3.0))
            * take_slice(curvature, 0, count_cells + 1, along_axis)
        )
    )
    upwind_minus = courant_faces * (
        take_slice(left_edge, 1, count_cells + 2, along_axis)
        - 0.5
        * courant_faces
        * (
            take_slice(slope_edge, 1, count_cells + 2, along_axis)
            + (1.0 + courant_faces * (2.0 / 3.0))
            * take_slice(curvature, 1, count_cells + 2, along_axis)
        )
    )
    face_flux = jnp.where(courant_faces > 0, upwind_plus, upwind_minus)
    return take_slice(face_flux, 0, count_cells, along_axis) - take_slice(
        face_flux, 1, count_cells + 1, along_axis
    )


def spectral_basis(blocks, block_len, span, mode_count):
    total_lon = blocks * block_len
    scale = 2.0 * math.pi / total_lon
    mode_index = jnp.arange(mode_count, dtype=jnp.int32)[None, :]
    coarse = jnp.arange(blocks, dtype=jnp.int32)[:, None]
    fine = jnp.arange(span, dtype=jnp.int32)[:, None]
    coarse_angle = ((block_len * coarse * mode_index) % total_lon).astype(jnp.float32) * scale
    fine_angle = ((fine * mode_index) % total_lon).astype(jnp.float32) * scale
    cc, sc = jnp.cos(coarse_angle)[:, None, :], jnp.sin(coarse_angle)[:, None, :]
    cf, sf = jnp.cos(fine_angle)[None], jnp.sin(fine_angle)[None]
    cosine = cc * cf - sc * sf
    sine = sc * cf + cc * sf
    table = jnp.concatenate([cosine, -sine], axis=2)
    mode_weight = (
        jnp.where((mode_index[0] == 0) | (2 * mode_index[0] == total_lon), 1.0, 2.0) / total_lon
    )
    return table, jnp.concatenate([mode_weight, mode_weight], axis=0)


def spectral_basis_by_mode(blocks, block_len, mode_count):
    total_lon = blocks * block_len
    scale = 2.0 * math.pi / total_lon
    mode_index = jnp.arange(mode_count, dtype=jnp.int32)[:, None]
    coarse = jnp.arange(blocks, dtype=jnp.int32)[None, :]
    fine = jnp.arange(block_len, dtype=jnp.int32)[None, :]
    coarse_angle = ((block_len * coarse * mode_index) % total_lon).astype(jnp.float32) * scale
    fine_angle = ((fine * mode_index) % total_lon).astype(jnp.float32) * scale
    cc, sc = jnp.cos(coarse_angle)[:, :, None], jnp.sin(coarse_angle)[:, :, None]
    cf, sf = jnp.cos(fine_angle)[:, None, :], jnp.sin(fine_angle)[:, None, :]
    cosine = cc * cf - sc * sf
    sine = sc * cf + cc * sf
    return jnp.concatenate([cosine, -sine], axis=0).reshape(2 * mode_count, total_lon)


def filter_correction(courant, row_factor):
    row_count, _, lon_local, levels = courant.shape
    blocks = lax.axis_size("lon")
    mode_count = row_factor.shape[1]
    per_device = 2 * row_count // blocks
    rows_here = per_device // 2
    table, mode_weight = spectral_basis(blocks, lon_local, lon_local + 1, mode_count)
    forward_table = spectral_basis_by_mode(blocks, lon_local, mode_count).astype(jnp.bfloat16)
    inverse_table = table.reshape(blocks * (lon_local + 1), 2 * mode_count).astype(jnp.bfloat16)
    outgoing = courant.transpose(0, 2, 1, 3).astype(jnp.bfloat16)
    outgoing = outgoing.reshape(blocks, rows_here * lon_local * 2, levels)
    pair_factor = jnp.repeat(1.0 - row_factor, 2, axis=0)
    removal = jnp.concatenate([pair_factor, pair_factor], axis=1) * mode_weight[None, :]
    arrived = lax.all_to_all(outgoing, "lon", split_axis=0, concat_axis=0, tiled=True)
    gathered = arrived.reshape(blocks, rows_here, lon_local, 2 * levels).transpose(0, 2, 1, 3)
    gathered = gathered.reshape(blocks * lon_local, rows_here * 2 * levels)
    first_row = lax.axis_index("lon") * per_device
    local_removal = lax.dynamic_slice_in_dim(removal, first_row, per_device, 0)
    spread_removal = jnp.repeat(local_removal.T, levels, axis=1)
    spectrum = jnp.dot(forward_table, gathered, preferred_element_type=jnp.float32)
    weighted = lax.optimization_barrier((spectrum * spread_removal).astype(jnp.bfloat16))
    correction = jnp.dot(inverse_table, weighted, preferred_element_type=jnp.float32)
    correction = correction.astype(jnp.bfloat16).reshape(blocks, lon_local + 1, rows_here, 2 * levels)
    correction = correction.transpose(0, 2, 1, 3)
    correction = correction.reshape(blocks, per_device * (lon_local + 1), levels)
    returned = lax.all_to_all(correction, "lon", split_axis=0, concat_axis=0, tiled=True)
    return returned.reshape(row_count, lon_local + 1, 2, levels)


def local(tracers, courant, row_mask, damped_modes, damping):
    rows_local = courant.shape[0]
    lon_local = courant.shape[2]
    mode_count = damping.shape[1]
    tracer_count = tracers.shape[0]
    lon_size = lax.axis_size("lon")
    mode_index = jnp.arange(mode_count, dtype=jnp.int32)
    damped = (row_mask[:, None] == 1) & (mode_index[None, :] >= mode_count - damped_modes[:, None])
    factor = jnp.where(damped, damping, 1.0)
    tracer_wide = padded(tracers, (("lon", 2),), 3, True).astype(jnp.float32)
    east_column = lax.ppermute(
        courant[:, 0, 0:1], "lon", [(i, (i - 1) % lon_size) for i in range(lon_size)]
    )
    correction = filter_correction(courant, factor).astype(jnp.float32)
    zonal_courant = jnp.concatenate([courant[:, 0], east_column], axis=1)
    zonal_faces = (zonal_courant - correction[:, :, 0]).astype(jnp.bfloat16)
    meridional_filtered = (courant[:, 1] - correction[:, :lon_local, 1]).astype(jnp.bfloat16)
    middle = (
        tracers.astype(jnp.float32)
        + ppm_change(tracer_wide, zonal_faces.astype(jnp.float32)[None], 2, lon_local)
    ).astype(jnp.bfloat16)
    meridional_stack = jnp.concatenate([middle, meridional_filtered[None]], axis=0)
    meridional_band = padded(meridional_stack, (("lat", 1),), 3, False)
    middle_wide = meridional_band[:tracer_count].astype(jnp.float32)
    meridional_faces = meridional_band[tracer_count, 3 : rows_local + 4].astype(jnp.float32)
    face_rows = lax.axis_index("lat") * rows_local + jnp.arange(rows_local + 1, dtype=jnp.int32)
    meridional_faces = jnp.where(face_rows[:, None, None] > 0, meridional_faces, 0.0)
    return (
        middle.astype(jnp.float32) + ppm_change(middle_wide, meridional_faces[None], 1, rows_local)
    ).astype(jnp.bfloat16)


def solution(mesh):
    placed = (
        P(None, "lat", "lon", None),
        P("lat", None, "lon", None),
        P("lat"),
        P("lat"),
        P("lat", None),
    )
    return jax.shard_map(
        local, mesh=mesh, in_specs=placed, out_specs=P(None, "lat", "lon", None), check_vma=False
    )
```

```python
import math

import jax
import jax.numpy as jnp
from jax import lax
from jax.experimental import pallas as pl
from jax.sharding import PartitionSpec as P


def padded(value, sides, width, wrap):
    for axis, dim in sides:
        size, length = (lax.axis_size(axis), value.shape[dim])
        up = [(i, (i + 1) % size) for i in range(size if wrap else size - 1)]
        down = [(j, i) for i, j in up]
        last = lax.slice_in_dim(value, length - width, length, axis=dim)
        leading = lax.slice_in_dim(value, 0, width, axis=dim)
        before = lax.ppermute(last, axis, up)
        after = lax.ppermute(leading, axis, down)
        value = jnp.concatenate([before, value, after], axis=dim)
    return value


def take_slice(values, low_end, high_end, along_axis):
    return lax.slice_in_dim(values, low_end, high_end, axis=along_axis)


def ppm_change(extended, courant_faces, along_axis, count_cells):
    edge_values = 7.0 / 12.0 * (
        take_slice(extended, 1, count_cells + 4, along_axis)
        + take_slice(extended, 2, count_cells + 5, along_axis)
    ) - 1.0 / 12.0 * (
        take_slice(extended, 0, count_cells + 3, along_axis)
        + take_slice(extended, 3, count_cells + 6, along_axis)
    )
    left_edge = take_slice(edge_values, 0, count_cells + 2, along_axis)
    right_edge = take_slice(edge_values, 1, count_cells + 3, along_axis)
    centre = take_slice(extended, 2, count_cells + 4, along_axis)
    slope_edge = right_edge - left_edge
    curvature = 6.0 * (centre - 0.5 * (left_edge + right_edge))
    upwind_plus = courant_faces * (
        take_slice(right_edge, 0, count_cells + 1, along_axis)
        - 0.5
        * courant_faces
        * (
            take_slice(slope_edge, 0, count_cells + 1, along_axis)
            - (1.0 - courant_faces * (2.0 / 3.0))
            * take_slice(curvature, 0, count_cells + 1, along_axis)
        )
    )
    upwind_minus = courant_faces * (
        take_slice(left_edge, 1, count_cells + 2, along_axis)
        - 0.5
        * courant_faces
        * (
            take_slice(slope_edge, 1, count_cells + 2, along_axis)
            + (1.0 + courant_faces * (2.0 / 3.0))
            * take_slice(curvature, 1, count_cells + 2, along_axis)
        )
    )
    face_flux = jnp.where(courant_faces > 0, upwind_plus, upwind_minus)
    return take_slice(face_flux, 0, count_cells, along_axis) - take_slice(
        face_flux, 1, count_cells + 1, along_axis
    )


def spectral_basis(blocks, block_len, span, mode_count):
    total_lon = blocks * block_len
    scale = 2.0 * math.pi / total_lon
    mode_index = jnp.arange(mode_count, dtype=jnp.int32)[None, :]
    coarse = jnp.arange(blocks, dtype=jnp.int32)[:, None]
    fine = jnp.arange(span, dtype=jnp.int32)[:, None]
    coarse_angle = ((block_len * coarse * mode_index) % total_lon).astype(jnp.float32) * scale
    fine_angle = ((fine * mode_index) % total_lon).astype(jnp.float32) * scale
    cc, sc = jnp.cos(coarse_angle)[:, None, :], jnp.sin(coarse_angle)[:, None, :]
    cf, sf = jnp.cos(fine_angle)[None], jnp.sin(fine_angle)[None]
    cosine = cc * cf - sc * sf
    sine = sc * cf + cc * sf
    table = jnp.concatenate([cosine, -sine], axis=2)
    mode_weight = (
        jnp.where((mode_index[0] == 0) | (2 * mode_index[0] == total_lon), 1.0, 2.0) / total_lon
    )
    return table, jnp.concatenate([mode_weight, mode_weight], axis=0)


def filter_correction(courant, row_factor):
    row_count, _, lon_local, levels = courant.shape
    blocks = lax.axis_size("lon")
    mode_count = row_factor.shape[1]
    per_device = 2 * row_count // blocks
    table, mode_weight = spectral_basis(blocks, lon_local, lon_local + 1, mode_count)
    forward_table = table[:, :lon_local].astype(jnp.bfloat16)
    inverse_table = table.astype(jnp.bfloat16)
    outgoing = courant.transpose(0, 2, 1, 3).astype(jnp.bfloat16)
    outgoing = outgoing.reshape(blocks, (2 * row_count // blocks) * lon_local, levels)
    pair_factor = jnp.repeat(1.0 - row_factor, 2, axis=0)
    removal = jnp.concatenate([pair_factor, pair_factor], axis=1) * mode_weight[None, :]
    arrived = lax.all_to_all(outgoing, "lon", split_axis=0, concat_axis=0, tiled=True)
    level_block = arrived.reshape(blocks, per_device // 2, lon_local, 2, levels)
    first_row = lax.axis_index("lon") * per_device
    local_removal = lax.dynamic_slice_in_dim(removal, first_row, per_device, 0)
    spectrum = jnp.einsum(
        "drjcl,djm->rcml", level_block, forward_table, preferred_element_type=jnp.float32
    ).reshape(per_device, 2 * mode_count, levels)
    weighted = (spectrum * local_removal[:, :, None]).astype(jnp.bfloat16)
    correction = jnp.einsum(
        "rcml,djm->drjcl",
        weighted.reshape(per_device // 2, 2, 2 * mode_count, levels),
        inverse_table,
        preferred_element_type=jnp.float32,
    ).astype(jnp.bfloat16)
    correction = correction.reshape(blocks, per_device * (lon_local + 1), levels)
    returned = lax.all_to_all(correction, "lon", split_axis=0, concat_axis=0, tiled=True)
    return returned.reshape(row_count, lon_local + 1, 2, levels)


def local(tracers, courant, row_mask, damped_modes, damping):
    rows_local = courant.shape[0]
    lon_local = courant.shape[2]
    mode_count = damping.shape[1]
    tracer_count = tracers.shape[0]
    lon_size = lax.axis_size("lon")
    mode_index = jnp.arange(mode_count, dtype=jnp.int32)
    damped = (row_mask[:, None] == 1) & (mode_index[None, :] >= mode_count - damped_modes[:, None])
    factor = jnp.where(damped, damping, 1.0)
    tracer_wide = padded(tracers, (("lon", 2),), 3, True).astype(jnp.float32)
    east_column = lax.ppermute(
        courant[:, 0, 0:1], "lon", [(i, (i - 1) % lon_size) for i in range(lon_size)]
    )
    correction = filter_correction(courant, factor).astype(jnp.float32)
    zonal_courant = jnp.concatenate([courant[:, 0], east_column], axis=1)
    zonal_faces = (zonal_courant - correction[:, :, 0]).astype(jnp.bfloat16)
    meridional_filtered = (courant[:, 1] - correction[:, :lon_local, 1]).astype(jnp.bfloat16)
    middle = (
        tracers.astype(jnp.float32)
        + ppm_change(tracer_wide, zonal_faces.astype(jnp.float32)[None], 2, lon_local)
    ).astype(jnp.bfloat16)
    meridional_stack = jnp.concatenate([middle, meridional_filtered[None]], axis=0)
    meridional_band = padded(meridional_stack, (("lat", 1),), 3, False)
    middle_wide = meridional_band[:tracer_count].astype(jnp.float32)
    meridional_faces = meridional_band[tracer_count, 3 : rows_local + 4].astype(jnp.float32)
    face_rows = lax.axis_index("lat") * rows_local + jnp.arange(rows_local + 1, dtype=jnp.int32)
    meridional_faces = jnp.where(face_rows[:, None, None] > 0, meridional_faces, 0.0)
    return meridional_step(middle_wide, meridional_faces[None], middle)


def meridional_kernel(wide_ref, faces_ref, middle_ref, out_ref):
    rows = out_ref.shape[1]
    change = ppm_change(wide_ref[0], faces_ref[0], 0, rows)
    out_ref[0] = (middle_ref[0].astype(jnp.float32) + change).astype(out_ref.dtype)


def meridional_step(middle_wide, meridional_faces, middle):
    return pl.pallas_call(
        meridional_kernel,
        out_shape=jax.ShapeDtypeStruct(middle.shape, middle.dtype),
        cost_estimate=pl.CostEstimate(
            flops=40 * middle.size, transcendentals=0, bytes_accessed=12 * middle.size
        ),
    )(middle_wide, meridional_faces, middle)


def solution(mesh):
    placed = (
        P(None, "lat", "lon", None),
        P("lat", None, "lon", None),
        P("lat"),
        P("lat"),
        P("lat", None),
    )
    return jax.shard_map(
        local, mesh=mesh, in_specs=placed, out_specs=P(None, "lat", "lon", None), check_vma=False
    )
```

```python
import math

import jax
import jax.numpy as jnp
from jax import lax
from jax.sharding import PartitionSpec as P


def padded(value, sides, width, wrap):
    for axis, dim in sides:
        size, length = (lax.axis_size(axis), value.shape[dim])
        up = [(i, (i + 1) % size) for i in range(size if wrap else size - 1)]
        down = [(j, i) for i, j in up]
        last = lax.slice_in_dim(value, length - width, length, axis=dim)
        leading = lax.slice_in_dim(value, 0, width, axis=dim)
        before = lax.ppermute(last, axis, up)
        after = lax.ppermute(leading, axis, down)
        value = jnp.concatenate([before, value, after], axis=dim)
    return value


def take_slice(values, low_end, high_end, along_axis):
    return lax.slice_in_dim(values, low_end, high_end, axis=along_axis)


def ppm_change(extended, courant_faces, along_axis, count_cells):
    edge_values = 7.0 / 12.0 * (
        take_slice(extended, 1, count_cells + 4, along_axis)
        + take_slice(extended, 2, count_cells + 5, along_axis)
    ) - 1.0 / 12.0 * (
        take_slice(extended, 0, count_cells + 3, along_axis)
        + take_slice(extended, 3, count_cells + 6, along_axis)
    )
    left_edge = take_slice(edge_values, 0, count_cells + 2, along_axis)
    right_edge = take_slice(edge_values, 1, count_cells + 3, along_axis)
    centre = take_slice(extended, 2, count_cells + 4, along_axis)
    slope_edge = right_edge - left_edge
    curvature = 6.0 * (centre - 0.5 * (left_edge + right_edge))
    upwind_plus = courant_faces * (
        take_slice(right_edge, 0, count_cells + 1, along_axis)
        - 0.5
        * courant_faces
        * (
            take_slice(slope_edge, 0, count_cells + 1, along_axis)
            - (1.0 - courant_faces * (2.0 / 3.0))
            * take_slice(curvature, 0, count_cells + 1, along_axis)
        )
    )
    upwind_minus = courant_faces * (
        take_slice(left_edge, 1, count_cells + 2, along_axis)
        - 0.5
        * courant_faces
        * (
            take_slice(slope_edge, 1, count_cells + 2, along_axis)
            + (1.0 + courant_faces * (2.0 / 3.0))
            * take_slice(curvature, 1, count_cells + 2, along_axis)
        )
    )
    face_flux = jnp.where(courant_faces > 0, upwind_plus, upwind_minus)
    return take_slice(face_flux, 0, count_cells, along_axis) - take_slice(
        face_flux, 1, count_cells + 1, along_axis
    )


def spectral_basis(blocks, block_len, span, mode_count):
    total_lon = blocks * block_len
    scale = 2.0 * math.pi / total_lon
    mode_index = jnp.arange(mode_count, dtype=jnp.int32)[None, :]
    coarse = jnp.arange(blocks, dtype=jnp.int32)[:, None]
    fine = jnp.arange(span, dtype=jnp.int32)[:, None]
    coarse_angle = ((block_len * coarse * mode_index) % total_lon).astype(jnp.float32) * scale
    fine_angle = ((fine * mode_index) % total_lon).astype(jnp.float32) * scale
    cc, sc = jnp.cos(coarse_angle)[:, None, :], jnp.sin(coarse_angle)[:, None, :]
    cf, sf = jnp.cos(fine_angle)[None], jnp.sin(fine_angle)[None]
    cosine = cc * cf - sc * sf
    sine = sc * cf + cc * sf
    table = jnp.concatenate([cosine, -sine], axis=2)
    mode_weight = (
        jnp.where((mode_index[0] == 0) | (2 * mode_index[0] == total_lon), 1.0, 2.0) / total_lon
    )
    return table, jnp.concatenate([mode_weight, mode_weight], axis=0)


def filter_correction(courant, row_factor):
    row_count, _, lon_local, levels = courant.shape
    blocks = lax.axis_size("lon")
    mode_count = row_factor.shape[1]
    per_device = 2 * row_count // blocks
    table, mode_weight = spectral_basis(blocks, lon_local, lon_local + 1, mode_count)
    forward_table = table[:, :lon_local].astype(jnp.bfloat16)
    inverse_table = table.astype(jnp.bfloat16)
    outgoing = courant.transpose(0, 2, 1, 3).astype(jnp.bfloat16)
    outgoing = outgoing.reshape(blocks, per_device // 2, lon_local, 2, levels)
    pair_factor = jnp.repeat(1.0 - row_factor, 2, axis=0)
    removal = jnp.concatenate([pair_factor, pair_factor], axis=1) * mode_weight[None, :]
    arrived = lax.all_to_all(outgoing, "lon", split_axis=0, concat_axis=0, tiled=True)
    level_block = arrived
    first_row = lax.axis_index("lon") * per_device
    local_removal = lax.dynamic_slice_in_dim(removal, first_row, per_device, 0)
    spectrum = jnp.einsum(
        "drjcl,djm->rcml", level_block, forward_table, preferred_element_type=jnp.float32
    ).reshape(per_device, 2 * mode_count, levels)
    weighted = lax.optimization_barrier((spectrum * local_removal[:, :, None]).astype(jnp.bfloat16))
    correction = jnp.einsum(
        "rcml,djm->drjcl",
        weighted.reshape(per_device // 2, 2, 2 * mode_count, levels),
        inverse_table,
        preferred_element_type=jnp.float32,
    ).astype(jnp.bfloat16)
    returned = lax.all_to_all(correction, "lon", split_axis=0, concat_axis=0, tiled=True)
    return returned.reshape(row_count, lon_local + 1, 2, levels)


def local(tracers, courant, row_mask, damped_modes, damping):
    rows_local = courant.shape[0]
    lon_local = courant.shape[2]
    mode_count = damping.shape[1]
    tracer_count = tracers.shape[0]
    lon_size = lax.axis_size("lon")
    mode_index = jnp.arange(mode_count, dtype=jnp.int32)
    damped = (row_mask[:, None] == 1) & (mode_index[None, :] >= mode_count - damped_modes[:, None])
    factor = jnp.where(damped, damping, 1.0)
    tracer_wide = padded(tracers, (("lon", 2),), 3, True).astype(jnp.float32)
    east_column = lax.ppermute(
        courant[:, 0, 0:1], "lon", [(i, (i - 1) % lon_size) for i in range(lon_size)]
    )
    correction = filter_correction(courant, factor).astype(jnp.float32)
    zonal_courant = jnp.concatenate([courant[:, 0], east_column], axis=1)
    zonal_faces = (zonal_courant - correction[:, :, 0]).astype(jnp.bfloat16)
    meridional_filtered = (courant[:, 1] - correction[:, :lon_local, 1]).astype(jnp.bfloat16)
    middle = (
        tracers.astype(jnp.float32)
        + ppm_change(tracer_wide, zonal_faces.astype(jnp.float32)[None], 2, lon_local)
    ).astype(jnp.bfloat16)
    meridional_stack = jnp.concatenate([middle, meridional_filtered[None]], axis=0)
    meridional_band = padded(meridional_stack, (("lat", 1),), 3, False)
    middle_wide = meridional_band[:tracer_count].astype(jnp.float32)
    meridional_faces = meridional_band[tracer_count, 3 : rows_local + 4].astype(jnp.float32)
    face_rows = lax.axis_index("lat") * rows_local + jnp.arange(rows_local + 1, dtype=jnp.int32)
    meridional_faces = jnp.where(face_rows[:, None, None] > 0, meridional_faces, 0.0)
    return (
        middle.astype(jnp.float32) + ppm_change(middle_wide, meridional_faces[None], 1, rows_local)
    ).astype(jnp.bfloat16)


def solution(mesh):
    placed = (
        P(None, "lat", "lon", None),
        P("lat", None, "lon", None),
        P("lat"),
        P("lat"),
        P("lat", None),
    )
    return jax.shard_map(
        local, mesh=mesh, in_specs=placed, out_specs=P(None, "lat", "lon", None), check_vma=False
    )
```

```python
import math

import jax
import jax.numpy as jnp
from jax import lax
from jax.sharding import PartitionSpec as P


def padded(value, sides, width, wrap):
    for axis, dim in sides:
        size, length = (lax.axis_size(axis), value.shape[dim])
        up = [(i, (i + 1) % size) for i in range(size if wrap else size - 1)]
        down = [(j, i) for i, j in up]
        last = lax.slice_in_dim(value, length - width, length, axis=dim)
        leading = lax.slice_in_dim(value, 0, width, axis=dim)
        before = lax.ppermute(last, axis, up)
        after = lax.ppermute(leading, axis, down)
        value = jnp.concatenate([before, value, after], axis=dim)
    return value


def take_slice(values, low_end, high_end, along_axis):
    return lax.slice_in_dim(values, low_end, high_end, axis=along_axis)


def ppm_change(extended, courant_faces, along_axis, count_cells):
    edge_values = 7.0 / 12.0 * (
        take_slice(extended, 1, count_cells + 4, along_axis)
        + take_slice(extended, 2, count_cells + 5, along_axis)
    ) - 1.0 / 12.0 * (
        take_slice(extended, 0, count_cells + 3, along_axis)
        + take_slice(extended, 3, count_cells + 6, along_axis)
    )
    left_edge = take_slice(edge_values, 0, count_cells + 2, along_axis)
    right_edge = take_slice(edge_values, 1, count_cells + 3, along_axis)
    centre = take_slice(extended, 2, count_cells + 4, along_axis)
    slope_edge = right_edge - left_edge
    curvature = 6.0 * (centre - 0.5 * (left_edge + right_edge))
    upwind_plus = courant_faces * (
        take_slice(right_edge, 0, count_cells + 1, along_axis)
        - 0.5
        * courant_faces
        * (
            take_slice(slope_edge, 0, count_cells + 1, along_axis)
            - (1.0 - courant_faces * (2.0 / 3.0))
            * take_slice(curvature, 0, count_cells + 1, along_axis)
        )
    )
    upwind_minus = courant_faces * (
        take_slice(left_edge, 1, count_cells + 2, along_axis)
        - 0.5
        * courant_faces
        * (
            take_slice(slope_edge, 1, count_cells + 2, along_axis)
            + (1.0 + courant_faces * (2.0 / 3.0))
            * take_slice(curvature, 1, count_cells + 2, along_axis)
        )
    )
    face_flux = jnp.where(courant_faces > 0, upwind_plus, upwind_minus)
    return take_slice(face_flux, 0, count_cells, along_axis) - take_slice(
        face_flux, 1, count_cells + 1, along_axis
    )


def spectral_basis(blocks, block_len, span, mode_count):
    total_lon = blocks * block_len
    scale = 2.0 * math.pi / total_lon
    mode_index = jnp.arange(mode_count, dtype=jnp.int32)[None, :]
    coarse = jnp.arange(blocks, dtype=jnp.int32)[:, None]
    fine = jnp.arange(span, dtype=jnp.int32)[:, None]
    coarse_angle = ((block_len * coarse * mode_index) % total_lon).astype(jnp.float32) * scale
    fine_angle = ((fine * mode_index) % total_lon).astype(jnp.float32) * scale
    cc, sc = jnp.cos(coarse_angle)[:, None, :], jnp.sin(coarse_angle)[:, None, :]
    cf, sf = jnp.cos(fine_angle)[None], jnp.sin(fine_angle)[None]
    cosine = cc * cf - sc * sf
    sine = sc * cf + cc * sf
    table = jnp.concatenate([cosine, -sine], axis=2)
    mode_weight = (
        jnp.where((mode_index[0] == 0) | (2 * mode_index[0] == total_lon), 1.0, 2.0) / total_lon
    )
    return table, jnp.concatenate([mode_weight, mode_weight], axis=0)


def filter_correction(courant, row_factor):
    row_count, _, lon_local, levels = courant.shape
    blocks = lax.axis_size("lon")
    mode_count = row_factor.shape[1]
    per_device = 2 * row_count // blocks
    rows_here = per_device // 2
    table, mode_weight = spectral_basis(blocks, lon_local, lon_local + 1, mode_count)
    forward_table = spectral_basis(blocks, lon_local, lon_local, mode_count)[0]
    forward_table = forward_table.reshape(blocks * lon_local, 2 * mode_count).astype(jnp.bfloat16)
    forward_table = lax.optimization_barrier(forward_table.T)
    inverse_table = table.astype(jnp.bfloat16)
    outgoing = courant.transpose(0, 2, 1, 3).astype(jnp.bfloat16)
    outgoing = outgoing.reshape(blocks, rows_here * lon_local * 2, levels)
    pair_factor = jnp.repeat(1.0 - row_factor, 2, axis=0)
    removal = jnp.concatenate([pair_factor, pair_factor], axis=1) * mode_weight[None, :]
    arrived = lax.all_to_all(outgoing, "lon", split_axis=0, concat_axis=0, tiled=True)
    gathered = arrived.reshape(blocks, rows_here, lon_local, 2 * levels).transpose(0, 2, 1, 3)
    gathered = gathered.reshape(blocks * lon_local, rows_here * 2 * levels)
    first_row = lax.axis_index("lon") * per_device
    local_removal = lax.dynamic_slice_in_dim(removal, first_row, per_device, 0)
    row_removal = local_removal.reshape(rows_here, 2, 2 * mode_count)[:, 0].T
    spectrum = jnp.dot(forward_table, gathered, preferred_element_type=jnp.float32)
    spectrum = spectrum.reshape(2 * mode_count, rows_here, 2 * levels)
    weighted = (spectrum * row_removal[:, :, None]).reshape(2 * mode_count, rows_here * 2 * levels)
    weighted = lax.optimization_barrier(weighted.astype(jnp.bfloat16))
    correction = jnp.einsum(
        "mk,djm->djk", weighted, inverse_table, preferred_element_type=jnp.float32
    ).astype(jnp.bfloat16)
    correction = correction.reshape(blocks, lon_local + 1, rows_here, 2 * levels)
    correction = correction.transpose(0, 2, 1, 3)
    correction = correction.reshape(blocks, per_device * (lon_local + 1), levels)
    returned = lax.all_to_all(correction, "lon", split_axis=0, concat_axis=0, tiled=True)
    return returned.reshape(row_count, lon_local + 1, 2, levels)


def local(tracers, courant, row_mask, damped_modes, damping):
    rows_local = courant.shape[0]
    lon_local = courant.shape[2]
    mode_count = damping.shape[1]
    tracer_count = tracers.shape[0]
    lon_size = lax.axis_size("lon")
    mode_index = jnp.arange(mode_count, dtype=jnp.int32)
    damped = (row_mask[:, None] == 1) & (mode_index[None, :] >= mode_count - damped_modes[:, None])
    factor = jnp.where(damped, damping, 1.0)
    tracer_wide = padded(tracers, (("lon", 2),), 3, True).astype(jnp.float32)
    east_column = lax.ppermute(
        courant[:, 0, 0:1], "lon", [(i, (i - 1) % lon_size) for i in range(lon_size)]
    )
    correction = filter_correction(courant, factor).astype(jnp.float32)
    zonal_courant = jnp.concatenate([courant[:, 0], east_column], axis=1)
    zonal_faces = (zonal_courant - correction[:, :, 0]).astype(jnp.bfloat16)
    meridional_filtered = (courant[:, 1] - correction[:, :lon_local, 1]).astype(jnp.bfloat16)
    middle = (
        tracers.astype(jnp.float32)
        + ppm_change(tracer_wide, zonal_faces.astype(jnp.float32)[None], 2, lon_local)
    ).astype(jnp.bfloat16)
    meridional_stack = jnp.concatenate([middle, meridional_filtered[None]], axis=0)
    meridional_band = padded(meridional_stack, (("lat", 1),), 3, False)
    middle_wide = meridional_band[:tracer_count].astype(jnp.float32)
    meridional_faces = meridional_band[tracer_count, 3 : rows_local + 4].astype(jnp.float32)
    face_rows = lax.axis_index("lat") * rows_local + jnp.arange(rows_local + 1, dtype=jnp.int32)
    meridional_faces = jnp.where(face_rows[:, None, None] > 0, meridional_faces, 0.0)
    return (
        middle.astype(jnp.float32) + ppm_change(middle_wide, meridional_faces[None], 1, rows_local)
    ).astype(jnp.bfloat16)


def solution(mesh):
    placed = (
        P(None, "lat", "lon", None),
        P("lat", None, "lon", None),
        P("lat"),
        P("lat"),
        P("lat", None),
    )
    return jax.shard_map(
        local, mesh=mesh, in_specs=placed, out_specs=P(None, "lat", "lon", None), check_vma=False
    )
```

```python
import math

import jax
import jax.numpy as jnp
from jax import lax
from jax.sharding import PartitionSpec as P


def padded(value, sides, width, wrap):
    for axis, dim in sides:
        size, length = (lax.axis_size(axis), value.shape[dim])
        up = [(i, (i + 1) % size) for i in range(size if wrap else size - 1)]
        down = [(j, i) for i, j in up]
        last = lax.slice_in_dim(value, length - width, length, axis=dim)
        leading = lax.slice_in_dim(value, 0, width, axis=dim)
        before = lax.ppermute(last, axis, up)
        after = lax.ppermute(leading, axis, down)
        value = jnp.concatenate([before, value, after], axis=dim)
    return value


def take_slice(values, low_end, high_end, along_axis):
    return lax.slice_in_dim(values, low_end, high_end, axis=along_axis)


def ppm_change(extended, courant_faces, along_axis, count_cells):
    edge_values = 7.0 / 12.0 * (
        take_slice(extended, 1, count_cells + 4, along_axis)
        + take_slice(extended, 2, count_cells + 5, along_axis)
    ) - 1.0 / 12.0 * (
        take_slice(extended, 0, count_cells + 3, along_axis)
        + take_slice(extended, 3, count_cells + 6, along_axis)
    )
    left_edge = take_slice(edge_values, 0, count_cells + 2, along_axis)
    right_edge = take_slice(edge_values, 1, count_cells + 3, along_axis)
    centre = take_slice(extended, 2, count_cells + 4, along_axis)
    slope_edge = right_edge - left_edge
    curvature = 6.0 * (centre - 0.5 * (left_edge + right_edge))
    upwind_plus = courant_faces * (
        take_slice(right_edge, 0, count_cells + 1, along_axis)
        - 0.5
        * courant_faces
        * (
            take_slice(slope_edge, 0, count_cells + 1, along_axis)
            - (1.0 - courant_faces * (2.0 / 3.0))
            * take_slice(curvature, 0, count_cells + 1, along_axis)
        )
    )
    upwind_minus = courant_faces * (
        take_slice(left_edge, 1, count_cells + 2, along_axis)
        - 0.5
        * courant_faces
        * (
            take_slice(slope_edge, 1, count_cells + 2, along_axis)
            + (1.0 + courant_faces * (2.0 / 3.0))
            * take_slice(curvature, 1, count_cells + 2, along_axis)
        )
    )
    face_flux = jnp.where(courant_faces > 0, upwind_plus, upwind_minus)
    return take_slice(face_flux, 0, count_cells, along_axis) - take_slice(
        face_flux, 1, count_cells + 1, along_axis
    )


def spectral_basis(blocks, block_len, span, mode_count):
    total_lon = blocks * block_len
    scale = 2.0 * math.pi / total_lon
    mode_index = jnp.arange(mode_count, dtype=jnp.int32)[None, :]
    coarse = jnp.arange(blocks, dtype=jnp.int32)[:, None]
    fine = jnp.arange(span, dtype=jnp.int32)[:, None]
    coarse_angle = ((block_len * coarse * mode_index) % total_lon).astype(jnp.float32) * scale
    fine_angle = ((fine * mode_index) % total_lon).astype(jnp.float32) * scale
    cc, sc = jnp.cos(coarse_angle)[:, None, :], jnp.sin(coarse_angle)[:, None, :]
    cf, sf = jnp.cos(fine_angle)[None], jnp.sin(fine_angle)[None]
    cosine = cc * cf - sc * sf
    sine = sc * cf + cc * sf
    table = jnp.concatenate([cosine, -sine], axis=2)
    mode_weight = (
        jnp.where((mode_index[0] == 0) | (2 * mode_index[0] == total_lon), 1.0, 2.0) / total_lon
    )
    return table, jnp.concatenate([mode_weight, mode_weight], axis=0)


def filter_correction(courant, row_factor):
    row_count, _, lon_local, levels = courant.shape
    blocks = lax.axis_size("lon")
    mode_count = row_factor.shape[1]
    table, mode_weight = spectral_basis(blocks, lon_local, lon_local + 1, mode_count)
    forward_table = table[:, :lon_local].reshape(blocks * lon_local, 2 * mode_count).astype(jnp.bfloat16)
    inverse_table = table.astype(jnp.bfloat16)
    flattened = courant.reshape(2 * row_count, lon_local, levels).astype(jnp.bfloat16)
    pair_factor = jnp.repeat(1.0 - row_factor, 2, axis=0)
    removal = jnp.concatenate([pair_factor, pair_factor], axis=1) * mode_weight[None, :]
    per_device = 2 * row_count // blocks
    level_block = lax.all_to_all(flattened, "lon", split_axis=0, concat_axis=1, tiled=True)
    first_row = lax.axis_index("lon") * per_device
    local_removal = lax.dynamic_slice_in_dim(removal, first_row, per_device, 0)
    spectrum = jnp.stack(
        [
            lax.dot_general(
                forward_table,
                level_block[c],
                (((0,), (0,)), ((), ())),
                preferred_element_type=jnp.float32,
            )
            for c in range(per_device)
        ]
    )
    weighted = (spectrum * local_removal[:, :, None]).astype(jnp.bfloat16)
    correction = jnp.einsum(
        "cml,djm->dcjl", weighted, inverse_table, preferred_element_type=jnp.float32
    ).astype(jnp.bfloat16)
    returned = lax.all_to_all(correction, "lon", split_axis=0, concat_axis=0, tiled=True)
    return returned.reshape(row_count, 2, lon_local + 1, levels)


def local(tracers, courant, row_mask, damped_modes, damping):
    rows_local = courant.shape[0]
    lon_local = courant.shape[2]
    mode_count = damping.shape[1]
    tracer_count = tracers.shape[0]
    lon_size = lax.axis_size("lon")
    mode_index = jnp.arange(mode_count, dtype=jnp.int32)
    damped = (row_mask[:, None] == 1) & (mode_index[None, :] >= mode_count - damped_modes[:, None])
    factor = jnp.where(damped, damping, 1.0)
    tracer_wide = padded(tracers, (("lon", 2),), 3, True).astype(jnp.float32)
    east_column = lax.ppermute(
        courant[:, 0, 0:1], "lon", [(i, (i - 1) % lon_size) for i in range(lon_size)]
    )
    correction = filter_correction(courant, factor).astype(jnp.float32)
    zonal_courant = jnp.concatenate([courant[:, 0], east_column], axis=1)
    zonal_faces = (zonal_courant - correction[:, 0]).astype(jnp.bfloat16)
    meridional_filtered = (courant[:, 1] - correction[:, 1, :lon_local]).astype(jnp.bfloat16)
    middle = (
        tracers.astype(jnp.float32)
        + ppm_change(tracer_wide, zonal_faces.astype(jnp.float32)[None], 2, lon_local)
    ).astype(jnp.bfloat16)
    meridional_stack = jnp.concatenate([middle, meridional_filtered[None]], axis=0)
    meridional_band = padded(meridional_stack, (("lat", 1),), 3, False)
    middle_wide = meridional_band[:tracer_count].astype(jnp.float32)
    meridional_faces = meridional_band[tracer_count, 3 : rows_local + 4].astype(jnp.float32)
    face_rows = lax.axis_index("lat") * rows_local + jnp.arange(rows_local + 1, dtype=jnp.int32)
    meridional_faces = jnp.where(face_rows[:, None, None] > 0, meridional_faces, 0.0)
    return (
        middle.astype(jnp.float32) + ppm_change(middle_wide, meridional_faces[None], 1, rows_local)
    ).astype(jnp.bfloat16)


def solution(mesh):
    placed = (
        P(None, "lat", "lon", None),
        P("lat", None, "lon", None),
        P("lat"),
        P("lat"),
        P("lat", None),
    )
    return jax.shard_map(
        local, mesh=mesh, in_specs=placed, out_specs=P(None, "lat", "lon", None), check_vma=False
    )
```

```python
import math

import jax
import jax.numpy as jnp
from jax import lax
from jax.sharding import PartitionSpec as P


def padded(value, sides, width, wrap):
    for axis, dim in sides:
        size, length = (lax.axis_size(axis), value.shape[dim])
        up = [(i, (i + 1) % size) for i in range(size if wrap else size - 1)]
        down = [(j, i) for i, j in up]
        last = lax.slice_in_dim(value, length - width, length, axis=dim)
        leading = lax.slice_in_dim(value, 0, width, axis=dim)
        before = lax.ppermute(last, axis, up)
        after = lax.ppermute(leading, axis, down)
        value = jnp.concatenate([before, value, after], axis=dim)
    return value


def take_slice(values, low_end, high_end, along_axis):
    return lax.slice_in_dim(values, low_end, high_end, axis=along_axis)


def ppm_change(extended, courant_faces, along_axis, count_cells):
    edge_values = 7.0 / 12.0 * (
        take_slice(extended, 1, count_cells + 4, along_axis)
        + take_slice(extended, 2, count_cells + 5, along_axis)
    ) - 1.0 / 12.0 * (
        take_slice(extended, 0, count_cells + 3, along_axis)
        + take_slice(extended, 3, count_cells + 6, along_axis)
    )
    left_edge = take_slice(edge_values, 0, count_cells + 2, along_axis)
    right_edge = take_slice(edge_values, 1, count_cells + 3, along_axis)
    centre = take_slice(extended, 2, count_cells + 4, along_axis)
    slope_edge = right_edge - left_edge
    curvature = 6.0 * (centre - 0.5 * (left_edge + right_edge))
    upwind_plus = courant_faces * (
        take_slice(right_edge, 0, count_cells + 1, along_axis)
        - 0.5
        * courant_faces
        * (
            take_slice(slope_edge, 0, count_cells + 1, along_axis)
            - (1.0 - courant_faces * (2.0 / 3.0))
            * take_slice(curvature, 0, count_cells + 1, along_axis)
        )
    )
    upwind_minus = courant_faces * (
        take_slice(left_edge, 1, count_cells + 2, along_axis)
        - 0.5
        * courant_faces
        * (
            take_slice(slope_edge, 1, count_cells + 2, along_axis)
            + (1.0 + courant_faces * (2.0 / 3.0))
            * take_slice(curvature, 1, count_cells + 2, along_axis)
        )
    )
    face_flux = jnp.where(courant_faces > 0, upwind_plus, upwind_minus)
    return take_slice(face_flux, 0, count_cells, along_axis) - take_slice(
        face_flux, 1, count_cells + 1, along_axis
    )


def spectral_basis(blocks, block_len, span, mode_count):
    total_lon = blocks * block_len
    scale = 2.0 * math.pi / total_lon
    mode_index = jnp.arange(mode_count, dtype=jnp.int32)[None, :]
    coarse = jnp.arange(blocks, dtype=jnp.int32)[:, None]
    fine = jnp.arange(span, dtype=jnp.int32)[:, None]
    coarse_angle = ((block_len * coarse * mode_index) % total_lon).astype(jnp.float32) * scale
    fine_angle = ((fine * mode_index) % total_lon).astype(jnp.float32) * scale
    cc, sc = jnp.cos(coarse_angle)[:, None, :], jnp.sin(coarse_angle)[:, None, :]
    cf, sf = jnp.cos(fine_angle)[None], jnp.sin(fine_angle)[None]
    cosine = cc * cf - sc * sf
    sine = sc * cf + cc * sf
    table = jnp.concatenate([cosine, -sine], axis=2)
    mode_weight = (
        jnp.where((mode_index[0] == 0) | (2 * mode_index[0] == total_lon), 1.0, 2.0) / total_lon
    )
    return table, jnp.concatenate([mode_weight, mode_weight], axis=0)


def filter_correction(courant, row_factor):
    row_count, _, lon_local, levels = courant.shape
    blocks = lax.axis_size("lon")
    mode_count = row_factor.shape[1]
    table, mode_weight = spectral_basis(blocks, lon_local, lon_local + 1, mode_count)
    forward_table = table[:, :lon_local].reshape(blocks * lon_local, 2 * mode_count).astype(jnp.bfloat16)
    inverse_table = table.astype(jnp.bfloat16)
    flattened = courant.reshape(2 * row_count, lon_local, levels).astype(jnp.bfloat16)
    pair_factor = jnp.repeat(1.0 - row_factor, 2, axis=0)
    removal = jnp.concatenate([pair_factor, pair_factor], axis=1) * mode_weight[None, :]
    per_device = 2 * row_count // blocks
    level_block = lax.all_to_all(flattened, "lon", split_axis=0, concat_axis=1, tiled=True)
    first_row = lax.axis_index("lon") * per_device
    local_removal = lax.dynamic_slice_in_dim(removal, first_row, per_device, 0)
    spectrum = jnp.einsum(
        "cnl,nm->cml", level_block, forward_table, preferred_element_type=jnp.float32
    )
    weighted = (spectrum * local_removal[:, :, None]).astype(jnp.bfloat16)
    correction = jnp.einsum(
        "cml,djm->dcjl", weighted, inverse_table, preferred_element_type=jnp.float32
    ).astype(jnp.bfloat16)
    returned = lax.all_to_all(correction, "lon", split_axis=0, concat_axis=0, tiled=True)
    return returned.reshape(row_count, 2, lon_local + 1, levels)


def local(tracers, courant, row_mask, damped_modes, damping):
    rows_local = courant.shape[0]
    lon_local = courant.shape[2]
    mode_count = damping.shape[1]
    tracer_count = tracers.shape[0]
    lon_size = lax.axis_size("lon")
    mode_index = jnp.arange(mode_count, dtype=jnp.int32)
    damped = (row_mask[:, None] == 1) & (mode_index[None, :] >= mode_count - damped_modes[:, None])
    factor = jnp.where(damped, damping, 1.0)
    tracer_wide = padded(tracers, (("lon", 2),), 3, True).astype(jnp.float32)
    east_column = lax.ppermute(
        courant[:, 0, 0:1], "lon", [(i, (i - 1) % lon_size) for i in range(lon_size)]
    )
    correction = filter_correction(courant, factor).astype(jnp.float32)
    zonal_courant = jnp.concatenate([courant[:, 0], east_column], axis=1)
    zonal_faces = (zonal_courant - correction[:, 0]).astype(jnp.bfloat16)
    meridional_filtered = (courant[:, 1] - correction[:, 1, :lon_local]).astype(jnp.bfloat16)
    middle = (
        tracers.astype(jnp.float32)
        + ppm_change(tracer_wide, zonal_faces.astype(jnp.float32)[None], 2, lon_local)
    ).astype(jnp.bfloat16)
    meridional_stack = jnp.concatenate([middle, meridional_filtered[None]], axis=0)
    meridional_band = padded(meridional_stack, (("lat", 1),), 3, False)
    middle_wide = meridional_band[:tracer_count].astype(jnp.float32)
    meridional_faces = meridional_band[tracer_count, 3 : rows_local + 4].astype(jnp.float32)
    face_rows = lax.axis_index("lat") * rows_local + jnp.arange(rows_local + 1, dtype=jnp.int32)
    meridional_faces = jnp.where(face_rows[:, None, None] > 0, meridional_faces, 0.0)
    middle_f32 = middle.astype(jnp.float32)
    faces = meridional_faces[None]

    inner_faces = meridional_filtered[None].astype(jnp.float32)

    def meridional_rows(low, high, wide, wide_low, row_faces, faces_low):
        cells = wide[:, low - wide_low : high - wide_low + 6]
        change = ppm_change(cells, row_faces[:, low - faces_low : high + 1 - faces_low], 1, high - low)
        return (middle_f32[:, low:high] + change).astype(jnp.bfloat16)

    inner = meridional_rows(3, rows_local - 3, middle_f32, 3, inner_faces, 0)
    top = meridional_rows(0, 3, middle_wide, 0, faces, 0)
    bottom = meridional_rows(rows_local - 3, rows_local, middle_wide, 0, faces, 0)
    return jnp.concatenate([top, inner, bottom], axis=1)


def solution(mesh):
    placed = (
        P(None, "lat", "lon", None),
        P("lat", None, "lon", None),
        P("lat"),
        P("lat"),
        P("lat", None),
    )
    return jax.shard_map(
        local, mesh=mesh, in_specs=placed, out_specs=P(None, "lat", "lon", None), check_vma=False
    )
```

```python
import math

import jax
import jax.numpy as jnp
from jax import lax
from jax.sharding import PartitionSpec as P


def padded(value, sides, width, wrap):
    for axis, dim in sides:
        size, length = (lax.axis_size(axis), value.shape[dim])
        up = [(i, (i + 1) % size) for i in range(size if wrap else size - 1)]
        down = [(j, i) for i, j in up]
        last = lax.slice_in_dim(value, length - width, length, axis=dim)
        leading = lax.slice_in_dim(value, 0, width, axis=dim)
        before = lax.ppermute(last, axis, up)
        after = lax.ppermute(leading, axis, down)
        value = jnp.concatenate([before, value, after], axis=dim)
    return value


def take_slice(values, low_end, high_end, along_axis):
    return lax.slice_in_dim(values, low_end, high_end, axis=along_axis)


def ppm_change(extended, courant_faces, along_axis, count_cells):
    edge_values = 7.0 / 12.0 * (
        take_slice(extended, 1, count_cells + 4, along_axis)
        + take_slice(extended, 2, count_cells + 5, along_axis)
    ) - 1.0 / 12.0 * (
        take_slice(extended, 0, count_cells + 3, along_axis)
        + take_slice(extended, 3, count_cells + 6, along_axis)
    )
    left_edge = take_slice(edge_values, 0, count_cells + 2, along_axis)
    right_edge = take_slice(edge_values, 1, count_cells + 3, along_axis)
    centre = take_slice(extended, 2, count_cells + 4, along_axis)
    slope_edge = right_edge - left_edge
    curvature = 6.0 * (centre - 0.5 * (left_edge + right_edge))
    upwind_plus = courant_faces * (
        take_slice(right_edge, 0, count_cells + 1, along_axis)
        - 0.5
        * courant_faces
        * (
            take_slice(slope_edge, 0, count_cells + 1, along_axis)
            - (1.0 - courant_faces * (2.0 / 3.0))
            * take_slice(curvature, 0, count_cells + 1, along_axis)
        )
    )
    upwind_minus = courant_faces * (
        take_slice(left_edge, 1, count_cells + 2, along_axis)
        - 0.5
        * courant_faces
        * (
            take_slice(slope_edge, 1, count_cells + 2, along_axis)
            + (1.0 + courant_faces * (2.0 / 3.0))
            * take_slice(curvature, 1, count_cells + 2, along_axis)
        )
    )
    face_flux = jnp.where(courant_faces > 0, upwind_plus, upwind_minus)
    return take_slice(face_flux, 0, count_cells, along_axis) - take_slice(
        face_flux, 1, count_cells + 1, along_axis
    )


def spectral_basis(blocks, block_len, span, mode_count):
    total_lon = blocks * block_len
    scale = 2.0 * math.pi / total_lon
    mode_index = jnp.arange(mode_count, dtype=jnp.int32)[None, :]
    coarse = jnp.arange(blocks, dtype=jnp.int32)[:, None]
    fine = jnp.arange(span, dtype=jnp.int32)[:, None]
    coarse_angle = ((block_len * coarse * mode_index) % total_lon).astype(jnp.float32) * scale
    fine_angle = ((fine * mode_index) % total_lon).astype(jnp.float32) * scale
    cc, sc = jnp.cos(coarse_angle)[:, None, :], jnp.sin(coarse_angle)[:, None, :]
    cf, sf = jnp.cos(fine_angle)[None], jnp.sin(fine_angle)[None]
    cosine = cc * cf - sc * sf
    sine = sc * cf + cc * sf
    table = jnp.concatenate([cosine, -sine], axis=2)
    mode_weight = (
        jnp.where((mode_index[0] == 0) | (2 * mode_index[0] == total_lon), 1.0, 2.0) / total_lon
    )
    return table, jnp.concatenate([mode_weight, mode_weight], axis=0)


def filter_correction(courant, row_factor):
    row_count, _, lon_local, levels = courant.shape
    blocks = lax.axis_size("lon")
    mode_count = row_factor.shape[1]
    table, mode_weight = spectral_basis(blocks, lon_local, lon_local + 1, mode_count)
    forward_table = table[:, :lon_local].reshape(blocks * lon_local, 2 * mode_count).astype(jnp.bfloat16)
    inverse_table = table.astype(jnp.bfloat16)
    flattened = courant.reshape(2 * row_count, lon_local, levels).astype(jnp.bfloat16)
    pair_factor = jnp.repeat(1.0 - row_factor, 2, axis=0)
    removal = jnp.concatenate([pair_factor, pair_factor], axis=1) * mode_weight[None, :]
    per_device = 2 * row_count // blocks
    level_block = lax.all_to_all(flattened, "lon", split_axis=0, concat_axis=1, tiled=True)
    first_row = lax.axis_index("lon") * per_device
    local_removal = lax.dynamic_slice_in_dim(removal, first_row, per_device, 0)
    spectrum = jnp.einsum(
        "cnl,nm->cml", level_block, forward_table, preferred_element_type=jnp.float32
    )
    weighted = (spectrum * local_removal[:, :, None]).astype(jnp.bfloat16)
    correction = jnp.einsum(
        "cml,djm->dcjl", weighted, inverse_table, preferred_element_type=jnp.float32
    ).astype(jnp.bfloat16)
    returned = lax.all_to_all(correction, "lon", split_axis=0, concat_axis=0, tiled=True)
    return returned.reshape(row_count, 2, lon_local + 1, levels)


def local(tracers, courant, row_mask, damped_modes, damping):
    rows_local = courant.shape[0]
    lon_local = courant.shape[2]
    mode_count = damping.shape[1]
    tracer_count = tracers.shape[0]
    lon_size = lax.axis_size("lon")
    mode_index = jnp.arange(mode_count, dtype=jnp.int32)
    damped = (row_mask[:, None] == 1) & (mode_index[None, :] >= mode_count - damped_modes[:, None])
    factor = jnp.where(damped, damping, 1.0)
    column = courant[None, :, 0, 0:1]
    column_high = column.astype(jnp.bfloat16)
    column_low = (column - column_high.astype(jnp.float32)).astype(jnp.bfloat16)
    westward = jnp.concatenate([tracers[:, :, 0:3], column_high, column_low], axis=2)
    eastward = tracers[:, :, lon_local - 3 :]
    from_east = lax.ppermute(westward, "lon", [(i, (i - 1) % lon_size) for i in range(lon_size)])
    from_west = lax.ppermute(eastward, "lon", [(i, (i + 1) % lon_size) for i in range(lon_size)])
    tracer_wide = jnp.concatenate([from_west, tracers, from_east[:, :, 0:3]], axis=2)
    tracer_wide = tracer_wide.astype(jnp.float32)
    east_column = from_east[0, :, 3:4].astype(jnp.float32) + from_east[0, :, 4:5].astype(jnp.float32)
    correction = filter_correction(courant, factor).astype(jnp.float32)
    zonal_courant = jnp.concatenate([courant[:, 0], east_column], axis=1)
    zonal_faces = (zonal_courant - correction[:, 0]).astype(jnp.bfloat16)
    meridional_filtered = (courant[:, 1] - correction[:, 1, :lon_local]).astype(jnp.bfloat16)
    middle = (
        tracers.astype(jnp.float32)
        + ppm_change(tracer_wide, zonal_faces.astype(jnp.float32)[None], 2, lon_local)
    ).astype(jnp.bfloat16)
    meridional_stack = jnp.concatenate([middle, meridional_filtered[None]], axis=0)
    meridional_band = padded(meridional_stack, (("lat", 1),), 3, False)
    middle_wide = meridional_band[:tracer_count].astype(jnp.float32)
    meridional_faces = meridional_band[tracer_count, 3 : rows_local + 4].astype(jnp.float32)
    face_rows = lax.axis_index("lat") * rows_local + jnp.arange(rows_local + 1, dtype=jnp.int32)
    meridional_faces = jnp.where(face_rows[:, None, None] > 0, meridional_faces, 0.0)
    return (
        middle.astype(jnp.float32) + ppm_change(middle_wide, meridional_faces[None], 1, rows_local)
    ).astype(jnp.bfloat16)


def solution(mesh):
    placed = (
        P(None, "lat", "lon", None),
        P("lat", None, "lon", None),
        P("lat"),
        P("lat"),
        P("lat", None),
    )
    return jax.shard_map(
        local, mesh=mesh, in_specs=placed, out_specs=P(None, "lat", "lon", None), check_vma=False
    )
```
